32 devices in a mesh: gz: 4 (over x, core), gy: 4 (over z), gx: 2 (over y).
Axes of the slice: x: 2, y: 2, z: 4, core: 2. Of those that a mesh axis runs over, the one named last changes fastest.
Arguments:
- volume: bfloat16 [32, 4, 32, 384], P('gz', 'gy', 'gx'), may hold values from -80 to 80
- cotangent: bfloat16 [32, 4, 32, 384], P('gz', 'gy', 'gx'), may hold values from -6 to 6
- w_project: bfloat16 [3, 384, 1152], P(None, 'gy', ('gz', 'gx')), may hold values from -0.3125 to 0.3125
- w_output: bfloat16 [3, 384, 384], P(None, 'gy', ('gz', 'gx')), may hold values from -0.3125 to 0.3125
Outputs:
- grad_volume: bfloat16 [32, 4, 32, 384], P('gz', 'gy', 'gx')
The draws below stay inside these ranges and needn't reach their ends.
All inputs are finite; a program needn't handle non-finite values.
Results may differ from the reference program's by a relative error of at most 0.015.
Values may be sent and summed in bfloat16 or wider, within the bound.
No kernel may reach another device: no remote copies, remote signals or barrier semaphores. Data moves between devices by JAX's collectives and lax.ppermute only.
A program may use at most 64 MiB of HBM per device.

```python
import math
import jax
import jax.numpy as jnp
from jax import lax

D = 384
HEADS = 6
Z = 32
Y = 4
X = 32


def draw_volume(key, part):
    base_key, row_key, col_key = jax.random.split(jax.random.fold_in(key, 7), 3)
    rough_part = jnp.clip(jax.random.normal(base_key, (Z, Y, X, D), jnp.float32), -4.0, 4.0)
    row_scale = jnp.exp(jax.random.uniform(row_key, (Z, Y, X, 1), jnp.float32, 0.0, math.log(10.0)))
    col_scale = jnp.exp(jax.random.uniform(col_key, (1, 1, 1, D), jnp.float32, -math.log(2.0), math.log(2.0)))
    return (rough_part * row_scale * col_scale).astype(jnp.bfloat16)


def levels(own_key, extent, shards, low, top_value):
    level, own = 1.0, jax.random.fold_in(own_key, 6)
    for axis_at, parts in shards:
        heights = jnp.exp(jax.random.uniform(jax.random.fold_in(own, axis_at), (parts,), jnp.float32, low / len(shards), top_value / len(shards)))
        level = level * jnp.repeat(heights, extent[axis_at] // parts).reshape([-1 if axis == axis_at else 1 for axis in range(len(extent))])
    return level


def noise(key, dims, width, limit, cuts=(), held_as=jnp.bfloat16):
    loudness = levels(key, dims, cuts, -0.22, 0.18) if cuts else 1.0
    values = jax.random.normal(key, dims, jnp.float32) * width * loudness
    return jnp.minimum(jnp.maximum(values, -limit), limit).astype(held_as)


def setup_inputs(seed: int = 0) -> dict:
    streams_of = jax.random.split(jax.random.key(seed), 5)
    volume = draw_volume(jax.random.fold_in(streams_of[4], 71), 0)
    cotangent = noise(streams_of[1], (Z, Y, X, D), 1.0, 6.0, ((0, 4), (1, 4), (2, 2)))
    w_project = noise(streams_of[2], (3, D, 3 * D), D ** -0.5, 0.3125, ((1, 4), (2, 8)))
    w_output = noise(streams_of[3], (3, D, D), D ** -0.5, 0.3125, ((1, 4), (2, 8)))
    return dict(volume=volume, cotangent=cotangent, w_project=w_project, w_output=w_output)


def head_norm(vector):
    return (vector * lax.rsqrt(lax.optimization_barrier(jnp.mean(vector * vector, axis=-1, keepdims=True)) + 1e-06)).astype(jnp.bfloat16)

def sublayer(line_rows, w_inner, w_outer):
    feat_len = line_rows.shape[-1]
    head_size = feat_len // HEADS
    stream = line_rows.astype(jnp.float32)
    normed = (stream * lax.rsqrt(lax.optimization_barrier(jnp.mean(stream * stream, axis=-1, keepdims=True)) + 1e-06)).astype(jnp.bfloat16)
    packed = jnp.dot(normed, w_inner, preferred_element_type=jnp.float32)
    head_shape = line_rows.shape[:3] + (HEADS, head_size)
    queries = head_norm(packed[..., :feat_len].reshape(head_shape))
    key_part = head_norm(packed[..., feat_len:2 * feat_len].reshape(head_shape))
    value_part = packed[..., 2 * feat_len:].reshape(head_shape).astype(jnp.bfloat16)
    scores = jnp.einsum('plqhe,pkqhe->pqhlk', queries.astype(jnp.float32), key_part.astype(jnp.float32)) * head_size ** (-0.5)
    powers = jnp.exp(scores)
    attn_weights = (powers / lax.optimization_barrier(jnp.sum(powers, axis=-1, keepdims=True))).astype(jnp.bfloat16)
    mixed_out = jnp.einsum('pqhlk,pkqhe->plqhe', attn_weights.astype(jnp.float32), value_part.astype(jnp.float32))
    mixed_out = mixed_out.astype(jnp.bfloat16).reshape(line_rows.shape)
    update = jnp.dot(mixed_out, w_outer, preferred_element_type=jnp.float32)
    return (stream + update).astype(jnp.bfloat16)

def along_axis(field, direction, w_inner, w_outer):
    if direction == 'depth':

        def one_slice(piece):
            return sublayer(piece[None], w_inner, w_outer)[0]
        moved = jnp.moveaxis(field, 1, 0)
        return jnp.moveaxis(lax.map(jax.checkpoint(one_slice), moved), 0, 1)
    if direction == 'rows':

        def one_slice(piece):
            return sublayer(piece[None], w_inner, w_outer)[0]
        return lax.map(jax.checkpoint(one_slice), field)

    def one_slice(piece):
        return sublayer(piece[:, :, None, :], w_inner, w_outer)[:, :, 0, :]
    return lax.map(jax.checkpoint(one_slice), field)

def reference(volume, cotangent, w_project, w_output):

    def forward(field):
        field = along_axis(field, 'depth', w_project[0], w_output[0])
        field = along_axis(field, 'rows', w_project[1], w_output[1])
        return along_axis(field, 'columns', w_project[2], w_output[2])
    _, pullback = jax.vjp(forward, volume)
    return pullback(cotangent)[0]
```

```python
import jax
import jax.numpy as jnp
from jax import lax
from jax.sharding import PartitionSpec as P

HEADS = 6
ALL = ("gz", "gy", "gx")


def head_norm(vector):
    return (vector * lax.rsqrt(jnp.mean(vector * vector, axis=-1, keepdims=True) + 1e-06)).astype(
        jnp.bfloat16
    )


def sublayer(line_rows, w_inner, w_outer):
    feat_len = line_rows.shape[-1]
    head_size = feat_len // HEADS
    stream = line_rows.astype(jnp.float32)
    normed = (stream * lax.rsqrt(jnp.mean(stream * stream, axis=-1, keepdims=True) + 1e-06)).astype(
        jnp.bfloat16
    )
    packed = jnp.dot(normed, w_inner, preferred_element_type=jnp.float32)
    head_shape = line_rows.shape[:3] + (HEADS, head_size)
    queries = head_norm(packed[..., :feat_len].reshape(head_shape))
    key_part = head_norm(packed[..., feat_len : 2 * feat_len].reshape(head_shape))
    value_part = packed[..., 2 * feat_len :].reshape(head_shape).astype(jnp.bfloat16)
    scores = jnp.einsum(
        "plqhe,pkqhe->pqhlk", queries, key_part, preferred_element_type=jnp.float32
    ) * head_size ** (-0.5)
    powers = jnp.exp(scores)
    attn_weights = (powers / jnp.sum(powers, axis=-1, keepdims=True)).astype(jnp.bfloat16)
    mixed_out = jnp.einsum(
        "pqhlk,pkqhe->plqhe", attn_weights, value_part, preferred_element_type=jnp.float32
    )
    mixed_out = mixed_out.astype(jnp.bfloat16).reshape(line_rows.shape)
    update = jnp.dot(mixed_out, w_outer, preferred_element_type=jnp.float32)
    return (stream + update).astype(jnp.bfloat16)


def full_weights(w_project, w_output, index, sizes):
    nz, ny, nx = sizes
    proj, outp = w_project[index], w_output[index]
    din, dproj = proj.shape
    cat = jnp.concatenate([proj, outp], axis=1)
    got = lax.all_gather(cat, ALL, axis=0, tiled=False)
    got = got.reshape(nz, ny, nx, din, cat.shape[1])
    got = jnp.transpose(got, (1, 3, 0, 2, 4)).reshape(ny * din, nz * nx, cat.shape[1])
    w_inner = got[:, :, :dproj].reshape(ny * din, nz * nx * dproj)
    w_outer = got[:, :, dproj:].reshape(ny * din, -1)
    return w_inner, w_outer


def depth_fn(member, w_inner, w_outer):
    depth_len, row_len, rest_len, feat_len = member.shape
    flat_lines = member.reshape(1, depth_len, row_len * rest_len, feat_len)
    return sublayer(flat_lines, w_inner, w_outer).reshape(member.shape)


def plane_fn(plane, w_row, w_col):
    after_rows = sublayer(plane[None], *w_row)[0]
    return sublayer(after_rows[:, :, None, :], *w_col)[:, :, 0, :]


def to_planes(depth_lines, sizes):
    nz, ny, nx = sizes
    z_len, yl, kx, feat = depth_lines.shape
    got = lax.all_to_all(depth_lines, ALL, 0, 0, tiled=True)
    got = got.reshape(nz, ny, nx, yl, kx, feat)
    return jnp.transpose(got, (1, 3, 2, 0, 4, 5)).reshape(ny * yl, nx * nz * kx, feat)


def from_planes(plane, sizes):
    nz, ny, nx = sizes
    rows, cols, feat = plane.shape
    yl, kx = rows // ny, cols // (nx * nz)
    parts = plane.reshape(ny, yl, nx, nz, kx, feat)
    parts = jnp.transpose(parts, (3, 0, 2, 1, 4, 5)).reshape(nz * ny * nx, yl, kx, feat)
    return lax.all_to_all(parts, ALL, 0, 0, tiled=True)


def block_to_plane(block, sizes):
    nz, ny, nx = sizes
    zl, yl, xl, feat = block.shape
    got = lax.all_to_all(block, ("gy", "gx"), 0, 0, tiled=True)
    got = got.reshape(ny, nx, yl, xl, feat)
    return jnp.transpose(got, (0, 2, 1, 3, 4)).reshape(ny * yl, nx * xl, feat)


def local(volume, cotangent, w_project, w_output, sizes):
    w_depth = full_weights(w_project, w_output, 0, sizes)
    w_row = full_weights(w_project, w_output, 1, sizes)
    w_col = full_weights(w_project, w_output, 2, sizes)

    depth_act = lax.all_to_all(volume, "gz", 2, 0, tiled=True)
    cot_plane = block_to_plane(cotangent, sizes)

    field_one, depth_pullback = jax.vjp(lambda m: depth_fn(m, *w_depth), depth_act)
    plane_one = to_planes(field_one, sizes)
    _, plane_pullback = jax.vjp(lambda p: plane_fn(p, w_row, w_col), plane_one)
    grad_plane = plane_pullback(cot_plane)[0]
    grad_one = from_planes(grad_plane, sizes)
    grad_zero = depth_pullback(grad_one)[0]
    return lax.all_to_all(grad_zero, "gz", 0, 2, tiled=True)


def along_rows(member, w_inner, w_outer):
    return sublayer(member, w_inner, w_outer)


def along_columns(member, w_inner, w_outer):
    depth_len, row_len, col_len, feat_len = member.shape
    flat_lines = member.reshape(depth_len * row_len, col_len, 1, feat_len)
    return sublayer(flat_lines, w_inner, w_outer).reshape(member.shape)


def line_swap(stacked, axis, split_axis, concat_axis):
    return lax.all_to_all(stacked, axis, split_axis=split_axis, concat_axis=concat_axis, tiled=True)


def local_general(volume, cotangent, w_project, w_output, sizes):
    w_depth = full_weights(w_project, w_output, 0, sizes)
    w_row = full_weights(w_project, w_output, 1, sizes)
    w_col = full_weights(w_project, w_output, 2, sizes)

    def row_fn(member):
        return along_rows(member, *w_row)

    def column_fn(member):
        return along_columns(member, *w_col)

    depth_act = line_swap(volume, "gz", 2, 0)
    field_one, depth_pullback = jax.vjp(lambda m: depth_fn(m, *w_depth), depth_act)
    field_one = line_swap(field_one, "gz", 0, 2)
    row_act = line_swap(field_one, "gy", 2, 1)
    field_two, row_pullback = jax.vjp(row_fn, row_act)
    field_two = line_swap(field_two, "gy", 1, 2)
    paired = line_swap(jnp.stack([cotangent, field_two]), "gx", 1, 3)
    _, column_pullback = jax.vjp(column_fn, paired[1])
    grad_two = line_swap(column_pullback(paired[0])[0], "gx", 2, 0)
    grad_one = line_swap(row_pullback(line_swap(grad_two, "gy", 2, 1))[0], "gy", 1, 2)
    grad_zero = depth_pullback(line_swap(grad_one, "gz", 2, 0))[0]
    return line_swap(grad_zero, "gz", 0, 2)


def solution(mesh):
    sizes = (mesh.shape["gz"], mesh.shape["gy"], mesh.shape["gx"])

    def body(volume, *rest):
        one_depth = volume.shape[0] * sizes[0] == mesh.size
        return (local if one_depth else local_general)(volume, *rest, sizes)

    return jax.shard_map(
        body,
        mesh=mesh,
        in_specs=(
            P("gz", "gy", "gx", None),
            P("gz", "gy", "gx", None),
            P(None, "gy", ("gz", "gx")),
            P(None, "gy", ("gz", "gx")),
        ),
        out_specs=P("gz", "gy", "gx", None),
        check_vma=False,
    )
```

```python
import jax
import jax.numpy as jnp
from jax import lax
from jax.sharding import PartitionSpec as P

HEADS = 6
HIGHEST = lax.Precision.HIGHEST
ALL = ("gz", "gy", "gx")


def head_map(feat_len):
    head_size = feat_len // HEADS
    return (jnp.arange(feat_len)[:, None] // head_size == jnp.arange(HEADS)[None, :]).astype(jnp.float32)


def head_norm(vector, ones):
    head_size = vector.shape[-1] // HEADS
    sums = jnp.dot(vector * vector, ones, precision=HIGHEST)
    scale = lax.rsqrt(sums / head_size + 1e-06)
    return (vector * jnp.dot(scale, ones.T, precision=HIGHEST)).astype(jnp.bfloat16)


def sublayer(line_rows, w_inner, w_outer):
    feat_len = line_rows.shape[-1]
    head_size = feat_len // HEADS
    ones = head_map(feat_len)
    mask = ones.T.astype(jnp.bfloat16)
    stream = line_rows.astype(jnp.float32)
    normed = (stream * lax.rsqrt(jnp.mean(stream * stream, axis=-1, keepdims=True) + 1e-06)).astype(jnp.bfloat16)
    packed = jnp.dot(normed, w_inner, preferred_element_type=jnp.float32)
    queries = head_norm(packed[..., :feat_len], ones)
    key_part = head_norm(packed[..., feat_len : 2 * feat_len], ones)
    value_part = packed[..., 2 * feat_len :].astype(jnp.bfloat16)
    key_heads = key_part[..., None, :] * mask
    scores = jnp.einsum("plqd,pkqhd->pqhlk", queries, key_heads, preferred_element_type=jnp.float32) * head_size ** (-0.5)
    powers = jnp.exp(scores)
    attn_weights = (powers / jnp.sum(powers, axis=-1, keepdims=True)).astype(jnp.bfloat16)
    mixed_heads = jnp.einsum("pqhlk,pkqd->plqhd", attn_weights, value_part, preferred_element_type=jnp.float32)
    mixed_out = jnp.sum(mixed_heads * mask.astype(jnp.float32), axis=-2).astype(jnp.bfloat16)
    update = jnp.dot(mixed_out, w_outer, preferred_element_type=jnp.float32)
    return (stream + update).astype(jnp.bfloat16)


def full_weights(w_project, w_output, sizes):
    nz, ny, nx = sizes
    subs, din, dproj = w_project.shape
    cat = jnp.concatenate([w_project, w_output], axis=2)
    got = lax.all_gather(cat, ALL, axis=0, tiled=False)
    got = got.reshape(nz, ny, nx, subs, din, cat.shape[2])
    got = jnp.transpose(got, (3, 1, 4, 0, 2, 5)).reshape(subs, ny * din, nz * nx, cat.shape[2])
    w_inner = got[:, :, :, :dproj].reshape(subs, ny * din, nz * nx * dproj)
    w_outer = got[:, :, :, dproj:].reshape(subs, ny * din, -1)
    return [(w_inner[i], w_outer[i]) for i in range(subs)]


def depth_fn(member, w_inner, w_outer):
    depth_len, row_len, rest_len, feat_len = member.shape
    flat_lines = member.reshape(1, depth_len, row_len * rest_len, feat_len)
    return sublayer(flat_lines, w_inner, w_outer).reshape(member.shape)


def plane_fn(plane, w_row, w_col):
    after_rows = sublayer(plane[None], *w_row)[0]
    return sublayer(after_rows[:, :, None, :], *w_col)[:, :, 0, :]


def to_planes(depth_lines, sizes):
    nz, ny, nx = sizes
    z_len, yl, kx, feat = depth_lines.shape
    got = lax.all_to_all(depth_lines, ALL, 0, 0, tiled=True)
    got = got.reshape(nz, ny, nx, yl, kx, feat)
    return jnp.transpose(got, (1, 3, 2, 0, 4, 5)).reshape(ny * yl, nx * nz * kx, feat)


def from_planes(plane, sizes):
    nz, ny, nx = sizes
    rows, cols, feat = plane.shape
    yl, kx = rows // ny, cols // (nx * nz)
    parts = plane.reshape(ny, yl, nx, nz, kx, feat)
    parts = jnp.transpose(parts, (3, 0, 2, 1, 4, 5)).reshape(nz * ny * nx, yl, kx, feat)
    return lax.all_to_all(parts, ALL, 0, 0, tiled=True)


def block_to_plane(block, sizes):
    nz, ny, nx = sizes
    zl, yl, xl, feat = block.shape
    got = lax.all_to_all(block, ("gy", "gx"), 0, 0, tiled=True)
    got = got.reshape(ny, nx, yl, xl, feat)
    return jnp.transpose(got, (0, 2, 1, 3, 4)).reshape(ny * yl, nx * xl, feat)


def local(volume, cotangent, w_project, w_output, sizes):
    w_depth, w_row, w_col = full_weights(w_project, w_output, sizes)

    depth_act = lax.all_to_all(volume, "gz", 2, 0, tiled=True)
    cot_plane = block_to_plane(cotangent, sizes)

    field_one, depth_pullback = jax.vjp(lambda m: depth_fn(m, *w_depth), depth_act)
    plane_one = to_planes(field_one, sizes)
    _, plane_pullback = jax.vjp(lambda p: plane_fn(p, w_row, w_col), plane_one)
    grad_plane = plane_pullback(cot_plane)[0]
    grad_one = from_planes(grad_plane, sizes)
    grad_zero = depth_pullback(grad_one)[0]
    return lax.all_to_all(grad_zero, "gz", 0, 2, tiled=True)


def along_rows(member, w_inner, w_outer):
    return sublayer(member, w_inner, w_outer)


def along_columns(member, w_inner, w_outer):
    depth_len, row_len, col_len, feat_len = member.shape
    flat_lines = member.reshape(depth_len * row_len, col_len, 1, feat_len)
    return sublayer(flat_lines, w_inner, w_outer).reshape(member.shape)


def line_swap(stacked, axis, split_axis, concat_axis):
    return lax.all_to_all(stacked, axis, split_axis=split_axis, concat_axis=concat_axis, tiled=True)


def local_general(volume, cotangent, w_project, w_output, sizes):
    w_depth, w_row, w_col = full_weights(w_project, w_output, sizes)

    def row_fn(member):
        return along_rows(member, *w_row)

    def column_fn(member):
        return along_columns(member, *w_col)

    depth_act = line_swap(volume, "gz", 2, 0)
    field_one, depth_pullback = jax.vjp(lambda m: depth_fn(m, *w_depth), depth_act)
    field_one = line_swap(field_one, "gz", 0, 2)
    row_act = line_swap(field_one, "gy", 2, 1)
    field_two, row_pullback = jax.vjp(row_fn, row_act)
    field_two = line_swap(field_two, "gy", 1, 2)
    paired = line_swap(jnp.stack([cotangent, field_two]), "gx", 1, 3)
    _, column_pullback = jax.vjp(column_fn, paired[1])
    grad_two = line_swap(column_pullback(paired[0])[0], "gx", 2, 0)
    grad_one = line_swap(row_pullback(line_swap(grad_two, "gy", 2, 1))[0], "gy", 1, 2)
    grad_zero = depth_pullback(line_swap(grad_one, "gz", 2, 0))[0]
    return line_swap(grad_zero, "gz", 0, 2)


def solution(mesh):
    sizes = (mesh.shape["gz"], mesh.shape["gy"], mesh.shape["gx"])

    def body(volume, *rest):
        one_depth = volume.shape[0] * sizes[0] == mesh.size
        return (local if one_depth else local_general)(volume, *rest, sizes)

    return jax.shard_map(
        body,
        mesh=mesh,
        in_specs=(
            P("gz", "gy", "gx", None),
            P("gz", "gy", "gx", None),
            P(None, "gy", ("gz", "gx")),
            P(None, "gy", ("gz", "gx")),
        ),
        out_specs=P("gz", "gy", "gx", None),
        check_vma=False,
    )
```

```python
import jax
import jax.numpy as jnp
from jax import lax
from jax.sharding import PartitionSpec as P

HEADS = 6
HIGHEST = lax.Precision.HIGHEST
ALL = ("gz", "gy", "gx")


def head_map(feat_len):
    head_size = feat_len // HEADS
    return (jnp.arange(feat_len)[:, None] // head_size == jnp.arange(HEADS)[None, :]).astype(jnp.float32)


def head_norm(vector, ones):
    head_size = vector.shape[-1] // HEADS
    sums = jnp.dot(vector * vector, ones, precision=HIGHEST)
    scale = lax.rsqrt(sums / head_size + 1e-06)
    return (vector * jnp.dot(scale, ones.T, precision=HIGHEST)).astype(jnp.bfloat16)


def sublayer(line_rows, w_inner, w_outer):
    feat_len = line_rows.shape[-1]
    head_size = feat_len // HEADS
    ones = head_map(feat_len)
    mask = ones.T.astype(jnp.bfloat16)
    stream = line_rows.astype(jnp.float32)
    normed = (stream * lax.rsqrt(jnp.mean(stream * stream, axis=-1, keepdims=True) + 1e-06)).astype(jnp.bfloat16)
    packed = jnp.dot(normed, w_inner, preferred_element_type=jnp.float32)
    queries = head_norm(packed[..., :feat_len], ones)
    key_part = head_norm(packed[..., feat_len : 2 * feat_len], ones)
    value_part = packed[..., 2 * feat_len :].astype(jnp.bfloat16)
    key_heads = key_part[..., None, :] * mask
    scores = jnp.einsum("plqd,pkqhd->pqhlk", queries, key_heads, preferred_element_type=jnp.float32) * head_size ** (-0.5)
    powers = jnp.exp(scores)
    attn_weights = (powers / jnp.sum(powers, axis=-1, keepdims=True)).astype(jnp.bfloat16)
    mixed_heads = jnp.einsum("pqhlk,pkqd->plqhd", attn_weights, value_part, preferred_element_type=jnp.float32)
    mixed_out = jnp.sum(mixed_heads * mask.astype(jnp.float32), axis=-2).astype(jnp.bfloat16)
    update = jnp.dot(mixed_out, w_outer, preferred_element_type=jnp.float32)
    return (stream + update).astype(jnp.bfloat16)


def arrange(got, sizes, dproj):
    nz, ny, nx = sizes
    subs, din, width = got.shape[1:]
    got = got.reshape(nz, ny, nx, subs, din, width)
    got = jnp.transpose(got, (3, 1, 4, 0, 2, 5)).reshape(subs, ny * din, nz * nx, width)
    w_inner = got[:, :, :, :dproj].reshape(subs, ny * din, nz * nx * dproj)
    w_outer = got[:, :, :, dproj:].reshape(subs, ny * din, -1)
    return [(w_inner[i], w_outer[i]) for i in range(subs)]


def full_weights(w_project, w_output, sizes):
    subs, din, dproj = w_project.shape
    cat = jnp.concatenate([w_project, w_output], axis=2)
    devices = sizes[0] * sizes[1] * sizes[2]
    first = jnp.broadcast_to(cat[:1][None], (devices,) + cat[:1].shape)
    first = lax.all_to_all(first, ALL, 0, 0, tiled=True)
    rest = lax.all_gather(cat[1:], ALL, axis=0, tiled=False)
    return arrange(first, sizes, dproj) + arrange(rest, sizes, dproj)


def depth_fn(member, w_inner, w_outer):
    depth_len, row_len, rest_len, feat_len = member.shape
    flat_lines = member.reshape(1, depth_len, row_len * rest_len, feat_len)
    return sublayer(flat_lines, w_inner, w_outer).reshape(member.shape)


def plane_fn(plane, w_row, w_col):
    after_rows = sublayer(plane[None], *w_row)[0]
    return sublayer(after_rows[:, :, None, :], *w_col)[:, :, 0, :]


def to_planes(depth_lines, sizes):
    nz, ny, nx = sizes
    z_len, yl, kx, feat = depth_lines.shape
    got = lax.all_to_all(depth_lines, ALL, 0, 0, tiled=True)
    got = got.reshape(nz, ny, nx, yl, kx, feat)
    return jnp.transpose(got, (1, 3, 2, 0, 4, 5)).reshape(ny * yl, nx * nz * kx, feat)


def from_planes(plane, sizes):
    nz, ny, nx = sizes
    rows, cols, feat = plane.shape
    yl, kx = rows // ny, cols // (nx * nz)
    parts = plane.reshape(ny, yl, nx, nz, kx, feat)
    parts = jnp.transpose(parts, (3, 0, 2, 1, 4, 5)).reshape(nz * ny * nx, yl, kx, feat)
    return lax.all_to_all(parts, ALL, 0, 0, tiled=True)


def block_to_plane(block, sizes):
    nz, ny, nx = sizes
    zl, yl, xl, feat = block.shape
    got = lax.all_to_all(block, ("gy", "gx"), 0, 0, tiled=True)
    got = got.reshape(ny, nx, yl, xl, feat)
    return jnp.transpose(got, (0, 2, 1, 3, 4)).reshape(ny * yl, nx * xl, feat)


def local(volume, cotangent, w_project, w_output, sizes):
    w_depth, w_row, w_col = full_weights(w_project, w_output, sizes)

    depth_act = lax.all_to_all(volume, "gz", 2, 0, tiled=True)
    cot_plane = block_to_plane(cotangent, sizes)

    field_one, depth_pullback = jax.vjp(lambda m: depth_fn(m, *w_depth), depth_act)
    plane_one = to_planes(field_one, sizes)
    _, plane_pullback = jax.vjp(lambda p: plane_fn(p, w_row, w_col), plane_one)
    grad_plane = plane_pullback(cot_plane)[0]
    grad_one = from_planes(grad_plane, sizes)
    grad_zero = depth_pullback(grad_one)[0]
    return lax.all_to_all(grad_zero, "gz", 0, 2, tiled=True)


def along_rows(member, w_inner, w_outer):
    return sublayer(member, w_inner, w_outer)


def along_columns(member, w_inner, w_outer):
    depth_len, row_len, col_len, feat_len = member.shape
    flat_lines = member.reshape(depth_len * row_len, col_len, 1, feat_len)
    return sublayer(flat_lines, w_inner, w_outer).reshape(member.shape)


def line_swap(stacked, axis, split_axis, concat_axis):
    return lax.all_to_all(stacked, axis, split_axis=split_axis, concat_axis=concat_axis, tiled=True)


def local_general(volume, cotangent, w_project, w_output, sizes):
    w_depth, w_row, w_col = full_weights(w_project, w_output, sizes)

    def row_fn(member):
        return along_rows(member, *w_row)

    def column_fn(member):
        return along_columns(member, *w_col)

    depth_act = line_swap(volume, "gz", 2, 0)
    field_one, depth_pullback = jax.vjp(lambda m: depth_fn(m, *w_depth), depth_act)
    field_one = line_swap(field_one, "gz", 0, 2)
    row_act = line_swap(field_one, "gy", 2, 1)
    field_two, row_pullback = jax.vjp(row_fn, row_act)
    field_two = line_swap(field_two, "gy", 1, 2)
    paired = line_swap(jnp.stack([cotangent, field_two]), "gx", 1, 3)
    _, column_pullback = jax.vjp(column_fn, paired[1])
    grad_two = line_swap(column_pullback(paired[0])[0], "gx", 2, 0)
    grad_one = line_swap(row_pullback(line_swap(grad_two, "gy", 2, 1))[0], "gy", 1, 2)
    grad_zero = depth_pullback(line_swap(grad_one, "gz", 2, 0))[0]
    return line_swap(grad_zero, "gz", 0, 2)


def solution(mesh):
    sizes = (mesh.shape["gz"], mesh.shape["gy"], mesh.shape["gx"])

    def body(volume, *rest):
        one_depth = volume.shape[0] * sizes[0] == mesh.size
        return (local if one_depth else local_general)(volume, *rest, sizes)

    return jax.shard_map(
        body,
        mesh=mesh,
        in_specs=(
            P("gz", "gy", "gx", None),
            P("gz", "gy", "gx", None),
            P(None, "gy", ("gz", "gx")),
            P(None, "gy", ("gz", "gx")),
        ),
        out_specs=P("gz", "gy", "gx", None),
        check_vma=False,
    )
```

```python
import jax
import jax.numpy as jnp
from jax import lax
from jax.sharding import PartitionSpec as P

HEADS = 6
HIGHEST = lax.Precision.HIGHEST
ALL = ("gz", "gy", "gx")


def head_map(feat_len):
    head_size = feat_len // HEADS
    return (jnp.arange(feat_len)[:, None] // head_size == jnp.arange(HEADS)[None, :]).astype(jnp.float32)


def head_norm(vector, ones):
    head_size = vector.shape[-1] // HEADS
    sums = jnp.dot(vector * vector, ones, precision=HIGHEST)
    scale = lax.rsqrt(sums / head_size + 1e-06)
    return (vector * jnp.dot(scale, ones.T, precision=HIGHEST)).astype(jnp.bfloat16)


def sublayer(line_rows, w_inner, w_outer):
    feat_len = line_rows.shape[-1]
    head_size = feat_len // HEADS
    ones = head_map(feat_len)
    mask = ones.T.astype(jnp.bfloat16)
    stream = line_rows.astype(jnp.float32)
    normed = (stream * lax.rsqrt(jnp.mean(stream * stream, axis=-1, keepdims=True) + 1e-06)).astype(jnp.bfloat16)
    packed = jnp.dot(normed, w_inner, preferred_element_type=jnp.float32)
    queries = head_norm(packed[..., :feat_len], ones)
    key_part = head_norm(packed[..., feat_len : 2 * feat_len], ones)
    value_part = packed[..., 2 * feat_len :].astype(jnp.bfloat16)
    key_heads = key_part[..., None, :] * mask
    scores = jnp.einsum("plqd,pkqhd->pqhlk", queries, key_heads, preferred_element_type=jnp.float32) * head_size ** (-0.5)
    powers = jnp.exp(scores)
    attn_weights = (powers / jnp.sum(powers, axis=-1, keepdims=True)).astype(jnp.bfloat16)
    mixed_heads = jnp.einsum("pqhlk,pkqd->plqhd", attn_weights, value_part, preferred_element_type=jnp.float32)
    mixed_out = jnp.sum(mixed_heads * mask.astype(jnp.float32), axis=-2).astype(jnp.bfloat16)
    update = jnp.dot(mixed_out, w_outer, preferred_element_type=jnp.float32)
    return (stream + update).astype(jnp.bfloat16)


def arrange(got, sizes, dproj):
    nz, ny, nx = sizes
    subs, din, width = got.shape[1:]
    got = got.reshape(nz, ny, nx, subs, din, width)
    got = jnp.transpose(got, (3, 1, 4, 0, 2, 5)).reshape(subs, ny * din, nz * nx, width)
    w_inner = got[:, :, :, :dproj].reshape(subs, ny * din, nz * nx * dproj)
    w_outer = got[:, :, :, dproj:].reshape(subs, ny * din, -1)
    return [(w_inner[i], w_outer[i]) for i in range(subs)]


def core_pairs(mesh):
    nz = mesh.shape["gz"]
    devices = list(mesh.devices.flat)
    count = len(devices)
    cores = [getattr(d, "core_on_chip", None) for d in devices]
    coords = [tuple(getattr(d, "coords", ())) for d in devices]
    if None not in cores and set(cores) == {0, 1}:
        place = {(coords[i], cores[i]): i for i in range(count)}
        partner = [place.get((coords[i], 1 - cores[i])) for i in range(count)]
        if None not in partner:
            return cores, partner
    if nz % 2:
        return None, None
    rest = count // nz
    cores = [(i // rest) % 2 for i in range(count)]
    partner = [i ^ rest if (i // rest) % 2 == 0 else i - rest for i in range(count)]
    return cores, partner


def gather_blocks(block, cores, partner, sizes):
    count = sizes[0] * sizes[1] * sizes[2]
    if cores is None:
        return lax.all_gather(block, ALL, axis=0, tiled=False)
    groups = [[i for i in range(count) if cores[i] == c] for c in (0, 1)]
    mine = lax.all_gather(block, ALL, axis=0, tiled=False, axis_index_groups=groups)
    other = lax.ppermute(mine, ALL, [(i, partner[i]) for i in range(count)])
    core = jnp.asarray(cores, jnp.int32)[lax.axis_index(ALL)]
    both = jnp.concatenate(
        [jnp.where(core == 0, mine, other), jnp.where(core == 0, other, mine)]
    )
    order = groups[0] + groups[1]
    nz = sizes[0]
    rest = count // nz
    swapped = [(2 * x + c) * rest + r for c in range(2) for x in range(nz // 2) for r in range(rest)]
    if order == swapped:
        both = both.reshape((2, nz // 2, count // nz) + block.shape)
        return jnp.swapaxes(both, 0, 1).reshape((count,) + block.shape)
    inverse = sorted(range(count), key=lambda i: order[i])
    return jnp.take(both, jnp.asarray(inverse, jnp.int32), axis=0)


def full_weights(w_project, w_output, sizes, pairs):
    subs, din, dproj = w_project.shape
    cat = jnp.concatenate([w_project, w_output], axis=2)
    return arrange(gather_blocks(cat, *pairs, sizes), sizes, dproj)


def depth_fn(member, w_inner, w_outer):
    depth_len, row_len, rest_len, feat_len = member.shape
    flat_lines = member.reshape(1, depth_len, row_len * rest_len, feat_len)
    return sublayer(flat_lines, w_inner, w_outer).reshape(member.shape)


def plane_fn(plane, w_row, w_col):
    after_rows = sublayer(plane[None], *w_row)[0]
    return sublayer(after_rows[:, :, None, :], *w_col)[:, :, 0, :]


def to_planes(depth_lines, sizes):
    nz, ny, nx = sizes
    z_len, yl, kx, feat = depth_lines.shape
    got = lax.all_to_all(depth_lines, ALL, 0, 0, tiled=True)
    got = got.reshape(nz, ny, nx, yl, kx, feat)
    return jnp.transpose(got, (1, 3, 2, 0, 4, 5)).reshape(ny * yl, nx * nz * kx, feat)


def from_planes(plane, sizes):
    nz, ny, nx = sizes
    rows, cols, feat = plane.shape
    yl, kx = rows // ny, cols // (nx * nz)
    parts = plane.reshape(ny, yl, nx, nz, kx, feat)
    parts = jnp.transpose(parts, (3, 0, 2, 1, 4, 5)).reshape(nz * ny * nx, yl, kx, feat)
    return lax.all_to_all(parts, ALL, 0, 0, tiled=True)


def block_to_plane(block, sizes):
    nz, ny, nx = sizes
    zl, yl, xl, feat = block.shape
    got = lax.all_to_all(block, ("gy", "gx"), 0, 0, tiled=True)
    got = got.reshape(ny, nx, yl, xl, feat)
    return jnp.transpose(got, (0, 2, 1, 3, 4)).reshape(ny * yl, nx * xl, feat)


def local(volume, cotangent, w_project, w_output, sizes, pairs):
    w_depth, w_row, w_col = full_weights(w_project, w_output, sizes, pairs)

    depth_act = lax.all_to_all(volume, "gz", 2, 0, tiled=True)
    cot_plane = block_to_plane(cotangent, sizes)

    field_one, depth_pullback = jax.vjp(lambda m: depth_fn(m, *w_depth), depth_act)
    plane_one = to_planes(field_one, sizes)
    _, plane_pullback = jax.vjp(lambda p: plane_fn(p, w_row, w_col), plane_one)
    grad_plane = plane_pullback(cot_plane)[0]
    grad_one = from_planes(grad_plane, sizes)
    grad_zero = depth_pullback(grad_one)[0]
    return lax.all_to_all(grad_zero, "gz", 0, 2, tiled=True)


def along_rows(member, w_inner, w_outer):
    return sublayer(member, w_inner, w_outer)


def along_columns(member, w_inner, w_outer):
    depth_len, row_len, col_len, feat_len = member.shape
    flat_lines = member.reshape(depth_len * row_len, col_len, 1, feat_len)
    return sublayer(flat_lines, w_inner, w_outer).reshape(member.shape)


def line_swap(stacked, axis, split_axis, concat_axis):
    return lax.all_to_all(stacked, axis, split_axis=split_axis, concat_axis=concat_axis, tiled=True)


def local_general(volume, cotangent, w_project, w_output, sizes, pairs):
    w_depth, w_row, w_col = full_weights(w_project, w_output, sizes, pairs)

    def row_fn(member):
        return along_rows(member, *w_row)

    def column_fn(member):
        return along_columns(member, *w_col)

    depth_act = line_swap(volume, "gz", 2, 0)
    field_one, depth_pullback = jax.vjp(lambda m: depth_fn(m, *w_depth), depth_act)
    field_one = line_swap(field_one, "gz", 0, 2)
    row_act = line_swap(field_one, "gy", 2, 1)
    field_two, row_pullback = jax.vjp(row_fn, row_act)
    field_two = line_swap(field_two, "gy", 1, 2)
    paired = line_swap(jnp.stack([cotangent, field_two]), "gx", 1, 3)
    _, column_pullback = jax.vjp(column_fn, paired[1])
    grad_two = line_swap(column_pullback(paired[0])[0], "gx", 2, 0)
    grad_one = line_swap(row_pullback(line_swap(grad_two, "gy", 2, 1))[0], "gy", 1, 2)
    grad_zero = depth_pullback(line_swap(grad_one, "gz", 2, 0))[0]
    return line_swap(grad_zero, "gz", 0, 2)


def solution(mesh):
    sizes = (mesh.shape["gz"], mesh.shape["gy"], mesh.shape["gx"])
    pairs = core_pairs(mesh)

    def body(volume, *rest):
        one_depth = volume.shape[0] * sizes[0] == mesh.size
        return (local if one_depth else local_general)(volume, *rest, sizes, pairs)

    return jax.shard_map(
        body,
        mesh=mesh,
        in_specs=(
            P("gz", "gy", "gx", None),
            P("gz", "gy", "gx", None),
            P(None, "gy", ("gz", "gx")),
            P(None, "gy", ("gz", "gx")),
        ),
        out_specs=P("gz", "gy", "gx", None),
        check_vma=False,
    )
```

```python
import jax
import jax.numpy as jnp
from jax import lax
from jax.sharding import PartitionSpec as P

HEADS = 6
HIGHEST = lax.Precision.HIGHEST
ALL = ("gz", "gy", "gx")


def head_map(feat_len):
    head_size = feat_len // HEADS
    return (jnp.arange(feat_len)[:, None] // head_size == jnp.arange(HEADS)[None, :]).astype(jnp.float32)


def head_norm(vector, ones):
    head_size = vector.shape[-1] // HEADS
    sums = jnp.dot(vector * vector, ones, precision=HIGHEST)
    scale = lax.rsqrt(sums / head_size + 1e-06)
    return (vector * jnp.dot(scale, ones.T, precision=HIGHEST)).astype(jnp.bfloat16)


def project(rows, weights, lo, hi):
    full = jnp.einsum("...d,acdn->...acn", rows, weights, preferred_element_type=jnp.float32)
    part = full[..., lo:hi]
    return part.reshape(part.shape[:-3] + (-1,))


def sublayer(line_rows, weights, dproj):
    feat_len = line_rows.shape[-1]
    head_size = feat_len // HEADS
    ones = head_map(feat_len)
    mask = ones.T.astype(jnp.bfloat16)
    stream = line_rows.astype(jnp.float32)
    normed = (stream * lax.rsqrt(jnp.mean(stream * stream, axis=-1, keepdims=True) + 1e-06)).astype(jnp.bfloat16)
    packed = project(normed, weights, 0, dproj)
    queries = head_norm(packed[..., :feat_len], ones)
    key_part = head_norm(packed[..., feat_len : 2 * feat_len], ones)
    value_part = packed[..., 2 * feat_len :].astype(jnp.bfloat16)
    key_heads = key_part[..., None, :] * mask
    scores = jnp.einsum("plqd,pkqhd->pqhlk", queries, key_heads, preferred_element_type=jnp.float32) * head_size ** (-0.5)
    powers = jnp.exp(scores)
    attn_weights = (powers / jnp.sum(powers, axis=-1, keepdims=True)).astype(jnp.bfloat16)
    mixed_heads = jnp.einsum("pqhlk,pkqd->plqhd", attn_weights, value_part, preferred_element_type=jnp.float32)
    mixed_out = jnp.sum(mixed_heads * mask.astype(jnp.float32), axis=-2).astype(jnp.bfloat16)
    update = project(mixed_out, weights, dproj, weights.shape[-1])
    return (stream + update).astype(jnp.bfloat16)


def full_weights(w_project, w_output, sizes):
    nz, ny, nx = sizes
    subs, din, dproj = w_project.shape
    cat = jnp.concatenate([w_project, w_output], axis=2)
    got = lax.all_gather(cat, ("gz", "gx", "gy"), axis=1, tiled=False)
    got = got.reshape(subs, nz, nx, ny * din, cat.shape[2])
    return [(got[i], dproj) for i in range(subs)]


def depth_fn(member, weights, dproj):
    depth_len, row_len, rest_len, feat_len = member.shape
    flat_lines = member.reshape(1, depth_len, row_len * rest_len, feat_len)
    return sublayer(flat_lines, weights, dproj).reshape(member.shape)


def plane_fn(plane, w_row, w_col):
    after_rows = sublayer(plane[None], *w_row)[0]
    return sublayer(after_rows[:, :, None, :], *w_col)[:, :, 0, :]


def to_planes(depth_lines, sizes):
    nz, ny, nx = sizes
    z_len, yl, kx, feat = depth_lines.shape
    got = lax.all_to_all(depth_lines, ALL, 0, 0, tiled=True)
    got = got.reshape(nz, ny, nx, yl, kx, feat)
    return jnp.transpose(got, (1, 3, 2, 0, 4, 5)).reshape(ny * yl, nx * nz * kx, feat)


def from_planes(plane, sizes):
    nz, ny, nx = sizes
    rows, cols, feat = plane.shape
    yl, kx = rows // ny, cols // (nx * nz)
    parts = plane.reshape(ny, yl, nx, nz, kx, feat)
    parts = jnp.transpose(parts, (3, 0, 2, 1, 4, 5)).reshape(nz * ny * nx, yl, kx, feat)
    return lax.all_to_all(parts, ALL, 0, 0, tiled=True)


def block_to_plane(block, sizes):
    nz, ny, nx = sizes
    zl, yl, xl, feat = block.shape
    got = lax.all_to_all(block, ("gy", "gx"), 0, 0, tiled=True)
    got = got.reshape(ny, nx, yl, xl, feat)
    return jnp.transpose(got, (0, 2, 1, 3, 4)).reshape(ny * yl, nx * xl, feat)


def local(volume, cotangent, w_project, w_output, sizes):
    w_depth, w_row, w_col = full_weights(w_project, w_output, sizes)

    depth_act = lax.all_to_all(volume, "gz", 2, 0, tiled=True)
    cot_plane = block_to_plane(cotangent, sizes)

    field_one, depth_pullback = jax.vjp(lambda m: depth_fn(m, *w_depth), depth_act)
    plane_one = to_planes(field_one, sizes)
    _, plane_pullback = jax.vjp(lambda p: plane_fn(p, w_row, w_col), plane_one)
    grad_plane = plane_pullback(cot_plane)[0]
    grad_one = from_planes(grad_plane, sizes)
    grad_zero = depth_pullback(grad_one)[0]
    return lax.all_to_all(grad_zero, "gz", 0, 2, tiled=True)


def along_rows(member, weights, dproj):
    return sublayer(member, weights, dproj)


def along_columns(member, weights, dproj):
    depth_len, row_len, col_len, feat_len = member.shape
    flat_lines = member.reshape(depth_len * row_len, col_len, 1, feat_len)
    return sublayer(flat_lines, weights, dproj).reshape(member.shape)


def line_swap(stacked, axis, split_axis, concat_axis):
    return lax.all_to_all(stacked, axis, split_axis=split_axis, concat_axis=concat_axis, tiled=True)


def local_general(volume, cotangent, w_project, w_output, sizes):
    w_depth, w_row, w_col = full_weights(w_project, w_output, sizes)

    def row_fn(member):
        return along_rows(member, *w_row)

    def column_fn(member):
        return along_columns(member, *w_col)

    depth_act = line_swap(volume, "gz", 2, 0)
    field_one, depth_pullback = jax.vjp(lambda m: depth_fn(m, *w_depth), depth_act)
    field_one = line_swap(field_one, "gz", 0, 2)
    row_act = line_swap(field_one, "gy", 2, 1)
    field_two, row_pullback = jax.vjp(row_fn, row_act)
    field_two = line_swap(field_two, "gy", 1, 2)
    paired = line_swap(jnp.stack([cotangent, field_two]), "gx", 1, 3)
    _, column_pullback = jax.vjp(column_fn, paired[1])
    grad_two = line_swap(column_pullback(paired[0])[0], "gx", 2, 0)
    grad_one = line_swap(row_pullback(line_swap(grad_two, "gy", 2, 1))[0], "gy", 1, 2)
    grad_zero = depth_pullback(line_swap(grad_one, "gz", 2, 0))[0]
    return line_swap(grad_zero, "gz", 0, 2)


def solution(mesh):
    sizes = (mesh.shape["gz"], mesh.shape["gy"], mesh.shape["gx"])

    def body(volume, *rest):
        one_depth = volume.shape[0] * sizes[0] == mesh.size
        return (local if one_depth else local_general)(volume, *rest, sizes)

    return jax.shard_map(
        body,
        mesh=mesh,
        in_specs=(
            P("gz", "gy", "gx", None),
            P("gz", "gy", "gx", None),
            P(None, "gy", ("gz", "gx")),
            P(None, "gy", ("gz", "gx")),
        ),
        out_specs=P("gz", "gy", "gx", None),
        check_vma=False,
    )
```

```python
import jax
import jax.numpy as jnp
from jax import lax
from jax.sharding import PartitionSpec as P

HEADS = 6
HIGHEST = lax.Precision.HIGHEST
ALL = ("gz", "gy", "gx")


def head_map(feat_len):
    head_size = feat_len // HEADS
    return (jnp.arange(feat_len)[:, None] // head_size == jnp.arange(HEADS)[None, :]).astype(jnp.float32)


def head_norm(vector, ones):
    head_size = vector.shape[-1] // HEADS
    sums = jnp.dot(vector * vector, ones, precision=HIGHEST)
    scale = lax.rsqrt(sums / head_size + 1e-06)
    return (vector * jnp.dot(scale, ones.T, precision=HIGHEST)).astype(jnp.bfloat16)


def sublayer(line_rows, w_inner, w_outer):
    feat_len = line_rows.shape[-1]
    head_size = feat_len // HEADS
    ones = head_map(feat_len)
    mask = ones.T.astype(jnp.bfloat16)
    stream = line_rows.astype(jnp.float32)
    normed = (stream * lax.rsqrt(jnp.mean(stream * stream, axis=-1, keepdims=True) + 1e-06)).astype(jnp.bfloat16)
    packed = jnp.dot(normed, w_inner, preferred_element_type=jnp.float32)
    queries = head_norm(packed[..., :feat_len], ones)
    key_part = head_norm(packed[..., feat_len : 2 * feat_len], ones)
    value_part = packed[..., 2 * feat_len :].astype(jnp.bfloat16)
    key_heads = key_part[..., None, :] * mask
    scores = jnp.einsum("plqd,pkqhd->pqhlk", queries, key_heads, preferred_element_type=jnp.float32) * head_size ** (-0.5)
    powers = jnp.exp(scores)
    attn_weights = (powers / jnp.sum(powers, axis=-1, keepdims=True)).astype(jnp.bfloat16)
    mixed_heads = jnp.einsum("pqhlk,pkqd->plqhd", attn_weights, value_part, preferred_element_type=jnp.float32)
    mixed_out = jnp.sum(mixed_heads * mask.astype(jnp.float32), axis=-2).astype(jnp.bfloat16)
    update = jnp.dot(mixed_out, w_outer, preferred_element_type=jnp.float32)
    return (stream + update).astype(jnp.bfloat16)


def full_weights(w_project, w_output, sizes):
    subs, din, dproj = w_project.shape
    cat = jnp.concatenate([w_project, w_output], axis=2)
    rows = lax.all_gather(cat, "gy", axis=1, tiled=True)
    proj = lax.all_gather(rows[:, :, :dproj], ("gz", "gx"), axis=2, tiled=True)
    outp = lax.all_gather(rows[:, :, dproj:], ("gz", "gx"), axis=2, tiled=True)
    return [(proj[i], outp[i]) for i in range(subs)]


def depth_fn(member, w_inner, w_outer):
    depth_len, row_len, rest_len, feat_len = member.shape
    flat_lines = member.reshape(1, depth_len, row_len * rest_len, feat_len)
    return sublayer(flat_lines, w_inner, w_outer).reshape(member.shape)


def plane_fn(plane, w_row, w_col):
    after_rows = sublayer(plane[None], *w_row)[0]
    return sublayer(after_rows[:, :, None, :], *w_col)[:, :, 0, :]


def to_planes(depth_lines, sizes):
    nz, ny, nx = sizes
    z_len, yl, kx, feat = depth_lines.shape
    got = lax.all_to_all(depth_lines, ALL, 0, 0, tiled=True)
    got = got.reshape(nz, ny, nx, yl, kx, feat)
    return jnp.transpose(got, (1, 3, 2, 0, 4, 5)).reshape(ny * yl, nx * nz * kx, feat)


def from_planes(plane, sizes):
    nz, ny, nx = sizes
    rows, cols, feat = plane.shape
    yl, kx = rows // ny, cols // (nx * nz)
    parts = plane.reshape(ny, yl, nx, nz, kx, feat)
    parts = jnp.transpose(parts, (3, 0, 2, 1, 4, 5)).reshape(nz * ny * nx, yl, kx, feat)
    return lax.all_to_all(parts, ALL, 0, 0, tiled=True)


def block_to_plane(block, sizes):
    nz, ny, nx = sizes
    zl, yl, xl, feat = block.shape
    got = lax.all_to_all(block, ("gy", "gx"), 0, 0, tiled=True)
    got = got.reshape(ny, nx, yl, xl, feat)
    return jnp.transpose(got, (0, 2, 1, 3, 4)).reshape(ny * yl, nx * xl, feat)


def local(volume, cotangent, w_project, w_output, sizes):
    w_depth, w_row, w_col = full_weights(w_project, w_output, sizes)

    depth_act = lax.all_to_all(volume, "gz", 2, 0, tiled=True)
    cot_plane = block_to_plane(cotangent, sizes)

    field_one, depth_pullback = jax.vjp(lambda m: depth_fn(m, *w_depth), depth_act)
    plane_one = to_planes(field_one, sizes)
    _, plane_pullback = jax.vjp(lambda p: plane_fn(p, w_row, w_col), plane_one)
    grad_plane = plane_pullback(cot_plane)[0]
    grad_one = from_planes(grad_plane, sizes)
    grad_zero = depth_pullback(grad_one)[0]
    return lax.all_to_all(grad_zero, "gz", 0, 2, tiled=True)


def along_rows(member, w_inner, w_outer):
    return sublayer(member, w_inner, w_outer)


def along_columns(member, w_inner, w_outer):
    depth_len, row_len, col_len, feat_len = member.shape
    flat_lines = member.reshape(depth_len * row_len, col_len, 1, feat_len)
    return sublayer(flat_lines, w_inner, w_outer).reshape(member.shape)


def line_swap(stacked, axis, split_axis, concat_axis):
    return lax.all_to_all(stacked, axis, split_axis=split_axis, concat_axis=concat_axis, tiled=True)


def local_general(volume, cotangent, w_project, w_output, sizes):
    w_depth, w_row, w_col = full_weights(w_project, w_output, sizes)

    def row_fn(member):
        return along_rows(member, *w_row)

    def column_fn(member):
        return along_columns(member, *w_col)

    depth_act = line_swap(volume, "gz", 2, 0)
    field_one, depth_pullback = jax.vjp(lambda m: depth_fn(m, *w_depth), depth_act)
    field_one = line_swap(field_one, "gz", 0, 2)
    row_act = line_swap(field_one, "gy", 2, 1)
    field_two, row_pullback = jax.vjp(row_fn, row_act)
    field_two = line_swap(field_two, "gy", 1, 2)
    paired = line_swap(jnp.stack([cotangent, field_two]), "gx", 1, 3)
    _, column_pullback = jax.vjp(column_fn, paired[1])
    grad_two = line_swap(column_pullback(paired[0])[0], "gx", 2, 0)
    grad_one = line_swap(row_pullback(line_swap(grad_two, "gy", 2, 1))[0], "gy", 1, 2)
    grad_zero = depth_pullback(line_swap(grad_one, "gz", 2, 0))[0]
    return line_swap(grad_zero, "gz", 0, 2)


def solution(mesh):
    sizes = (mesh.shape["gz"], mesh.shape["gy"], mesh.shape["gx"])

    def body(volume, *rest):
        one_depth = volume.shape[0] * sizes[0] == mesh.size
        return (local if one_depth else local_general)(volume, *rest, sizes)

    return jax.shard_map(
        body,
        mesh=mesh,
        in_specs=(
            P("gz", "gy", "gx", None),
            P("gz", "gy", "gx", None),
            P(None, "gy", ("gz", "gx")),
            P(None, "gy", ("gz", "gx")),
        ),
        out_specs=P("gz", "gy", "gx", None),
        check_vma=False,
    )
```

```python
import jax
import jax.numpy as jnp
from jax import lax
from jax.sharding import PartitionSpec as P

HEADS = 6
HIGHEST = lax.Precision.HIGHEST
ALL = ("gz", "gy", "gx")


def head_map(feat_len):
    head_size = feat_len // HEADS
    return (jnp.arange(feat_len)[:, None] // head_size == jnp.arange(HEADS)[None, :]).astype(jnp.float32)


def head_norm(vector, ones):
    head_size = vector.shape[-1] // HEADS
    sums = jnp.dot(vector * vector, ones, precision=HIGHEST)
    scale = lax.rsqrt(sums / head_size + 1e-06)
    return (vector * jnp.dot(scale, ones.T, precision=HIGHEST)).astype(jnp.bfloat16)


def sublayer(line_rows, w_inner, w_outer):
    feat_len = line_rows.shape[-1]
    head_size = feat_len // HEADS
    ones = head_map(feat_len)
    mask = ones.T.astype(jnp.bfloat16)
    stream = line_rows.astype(jnp.float32)
    normed = (stream * lax.rsqrt(jnp.mean(stream * stream, axis=-1, keepdims=True) + 1e-06)).astype(jnp.bfloat16)
    packed = jnp.dot(normed, w_inner, preferred_element_type=jnp.float32)
    queries = head_norm(packed[..., :feat_len], ones)
    key_part = head_norm(packed[..., feat_len : 2 * feat_len], ones)
    value_part = packed[..., 2 * feat_len :].astype(jnp.bfloat16)
    key_heads = key_part[..., None, :] * mask
    scores = jnp.einsum("plqd,pkqhd->pqhlk", queries, key_heads, preferred_element_type=jnp.float32) * head_size ** (-0.5)
    powers = jnp.exp(scores)
    attn_weights = (powers / jnp.sum(powers, axis=-1, keepdims=True)).astype(jnp.bfloat16)
    mixed_heads = jnp.einsum("pqhlk,pkqd->plqhd", attn_weights, value_part, preferred_element_type=jnp.float32)
    mixed_out = jnp.sum(mixed_heads * mask.astype(jnp.float32), axis=-2).astype(jnp.bfloat16)
    update = jnp.dot(mixed_out, w_outer, preferred_element_type=jnp.float32)
    return (stream + update).astype(jnp.bfloat16)


def full_weights(w_project, w_output, sizes):
    subs, din, dproj = w_project.shape
    cat = jnp.concatenate([w_project, w_output], axis=2)
    ny = sizes[1]
    rows = lax.all_to_all(jnp.broadcast_to(cat[None], (ny,) + cat.shape), "gy", 0, 0, tiled=True)
    rows = jnp.swapaxes(rows, 0, 1).reshape(subs, ny * din, cat.shape[2])
    proj = lax.all_gather(rows[:, :, :dproj], ("gz", "gx"), axis=2, tiled=True)
    outp = lax.all_gather(rows[:, :, dproj:], ("gz", "gx"), axis=2, tiled=True)
    return [(proj[i], outp[i]) for i in range(subs)]


def depth_fn(member, w_inner, w_outer):
    depth_len, row_len, rest_len, feat_len = member.shape
    flat_lines = member.reshape(1, depth_len, row_len * rest_len, feat_len)
    return sublayer(flat_lines, w_inner, w_outer).reshape(member.shape)


def plane_fn(plane, w_row, w_col):
    after_rows = sublayer(plane[None], *w_row)[0]
    return sublayer(after_rows[:, :, None, :], *w_col)[:, :, 0, :]


def to_planes(depth_lines, sizes):
    nz, ny, nx = sizes
    z_len, yl, kx, feat = depth_lines.shape
    got = lax.all_to_all(depth_lines, ALL, 0, 0, tiled=True)
    got = got.reshape(nz, ny, nx, yl, kx, feat)
    return jnp.transpose(got, (1, 3, 2, 0, 4, 5)).reshape(ny * yl, nx * nz * kx, feat)


def from_planes(plane, sizes):
    nz, ny, nx = sizes
    rows, cols, feat = plane.shape
    yl, kx = rows // ny, cols // (nx * nz)
    parts = plane.reshape(ny, yl, nx, nz, kx, feat)
    parts = jnp.transpose(parts, (3, 0, 2, 1, 4, 5)).reshape(nz * ny * nx, yl, kx, feat)
    return lax.all_to_all(parts, ALL, 0, 0, tiled=True)


def block_to_plane(block, sizes):
    nz, ny, nx = sizes
    zl, yl, xl, feat = block.shape
    got = lax.all_to_all(block, ("gy", "gx"), 0, 0, tiled=True)
    got = got.reshape(ny, nx, yl, xl, feat)
    return jnp.transpose(got, (0, 2, 1, 3, 4)).reshape(ny * yl, nx * xl, feat)


def local(volume, cotangent, w_project, w_output, sizes):
    w_depth, w_row, w_col = full_weights(w_project, w_output, sizes)

    depth_act = lax.all_to_all(volume, "gz", 2, 0, tiled=True)
    cot_plane = block_to_plane(cotangent, sizes)

    field_one, depth_pullback = jax.vjp(lambda m: depth_fn(m, *w_depth), depth_act)
    plane_one = to_planes(field_one, sizes)
    _, plane_pullback = jax.vjp(lambda p: plane_fn(p, w_row, w_col), plane_one)
    grad_plane = plane_pullback(cot_plane)[0]
    grad_one = from_planes(grad_plane, sizes)
    grad_zero = depth_pullback(grad_one)[0]
    return lax.all_to_all(grad_zero, "gz", 0, 2, tiled=True)


def along_rows(member, w_inner, w_outer):
    return sublayer(member, w_inner, w_outer)


def along_columns(member, w_inner, w_outer):
    depth_len, row_len, col_len, feat_len = member.shape
    flat_lines = member.reshape(depth_len * row_len, col_len, 1, feat_len)
    return sublayer(flat_lines, w_inner, w_outer).reshape(member.shape)


def line_swap(stacked, axis, split_axis, concat_axis):
    return lax.all_to_all(stacked, axis, split_axis=split_axis, concat_axis=concat_axis, tiled=True)


def local_general(volume, cotangent, w_project, w_output, sizes):
    w_depth, w_row, w_col = full_weights(w_project, w_output, sizes)

    def row_fn(member):
        return along_rows(member, *w_row)

    def column_fn(member):
        return along_columns(member, *w_col)

    depth_act = line_swap(volume, "gz", 2, 0)
    field_one, depth_pullback = jax.vjp(lambda m: depth_fn(m, *w_depth), depth_act)
    field_one = line_swap(field_one, "gz", 0, 2)
    row_act = line_swap(field_one, "gy", 2, 1)
    field_two, row_pullback = jax.vjp(row_fn, row_act)
    field_two = line_swap(field_two, "gy", 1, 2)
    paired = line_swap(jnp.stack([cotangent, field_two]), "gx", 1, 3)
    _, column_pullback = jax.vjp(column_fn, paired[1])
    grad_two = line_swap(column_pullback(paired[0])[0], "gx", 2, 0)
    grad_one = line_swap(row_pullback(line_swap(grad_two, "gy", 2, 1))[0], "gy", 1, 2)
    grad_zero = depth_pullback(line_swap(grad_one, "gz", 2, 0))[0]
    return line_swap(grad_zero, "gz", 0, 2)


def solution(mesh):
    sizes = (mesh.shape["gz"], mesh.shape["gy"], mesh.shape["gx"])

    def body(volume, *rest):
        one_depth = volume.shape[0] * sizes[0] == mesh.size
        return (local if one_depth else local_general)(volume, *rest, sizes)

    return jax.shard_map(
        body,
        mesh=mesh,
        in_specs=(
            P("gz", "gy", "gx", None),
            P("gz", "gy", "gx", None),
            P(None, "gy", ("gz", "gx")),
            P(None, "gy", ("gz", "gx")),
        ),
        out_specs=P("gz", "gy", "gx", None),
        check_vma=False,
    )
```

```python
import jax
import jax.numpy as jnp
from jax import lax
from jax.sharding import PartitionSpec as P

HEADS = 6
HIGHEST = lax.Precision.HIGHEST
ALL = ("gz", "gy", "gx")


def head_map(feat_len):
    head_size = feat_len // HEADS
    return (jnp.arange(feat_len)[:, None] // head_size == jnp.arange(HEADS)[None, :]).astype(jnp.float32)


def head_norm(vector, ones):
    head_size = vector.shape[-1] // HEADS
    sums = jnp.dot(vector * vector, ones, precision=HIGHEST)
    scale = lax.rsqrt(sums / head_size + 1e-06)
    return (vector * jnp.dot(scale, ones.T, precision=HIGHEST)).astype(jnp.bfloat16)


def sublayer(line_rows, w_inner, w_outer):
    feat_len = line_rows.shape[-1]
    head_size = feat_len // HEADS
    ones = head_map(feat_len)
    mask = ones.T.astype(jnp.bfloat16)
    stream = line_rows.astype(jnp.float32)
    normed = (stream * lax.rsqrt(jnp.mean(stream * stream, axis=-1, keepdims=True) + 1e-06)).astype(jnp.bfloat16)
    packed = jnp.dot(normed, w_inner, preferred_element_type=jnp.float32)
    queries = head_norm(packed[..., :feat_len], ones)
    key_part = head_norm(packed[..., feat_len : 2 * feat_len], ones)
    value_part = packed[..., 2 * feat_len :].astype(jnp.bfloat16)
    key_heads = key_part[..., None, :] * mask
    scores = jnp.einsum("plqd,pkqhd->pqhlk", queries, key_heads, preferred_element_type=jnp.float32) * head_size ** (-0.5)
    powers = jnp.exp(scores)
    attn_weights = (powers / jnp.sum(powers, axis=-1, keepdims=True)).astype(jnp.bfloat16)
    mixed_heads = jnp.einsum("pqhlk,pkqd->plqhd", attn_weights, value_part, preferred_element_type=jnp.float32)
    mixed_out = jnp.sum(mixed_heads * mask.astype(jnp.float32), axis=-2).astype(jnp.bfloat16)
    update = jnp.dot(mixed_out, w_outer, preferred_element_type=jnp.float32)
    return (stream + update).astype(jnp.bfloat16)


def full_weights(w_project, w_output, sizes):
    subs, din, dproj = w_project.shape
    dout = w_output.shape[2]
    blocks = sizes[0] * sizes[2]
    cat = jnp.concatenate([w_project, w_output], axis=2)
    rows = lax.all_gather(cat, "gy", axis=1, tiled=True)
    feat = rows.shape[1]
    weights = []
    for index in range(subs):
        proj, outp = rows[index, :, :dproj], rows[index, :, dproj:]
        stacked = jnp.concatenate([proj, outp.reshape(-1, dproj)], axis=0)
        got = lax.all_gather(stacked, ("gz", "gx"), axis=1, tiled=True)
        w_inner = got[:feat]
        w_outer = got[feat:].reshape(-1, blocks, dproj).swapaxes(0, 1).reshape(blocks, feat, dout)
        weights.append((w_inner, w_outer.swapaxes(0, 1).reshape(feat, blocks * dout)))
    return weights


def depth_fn(member, w_inner, w_outer):
    depth_len, row_len, rest_len, feat_len = member.shape
    flat_lines = member.reshape(1, depth_len, row_len * rest_len, feat_len)
    return sublayer(flat_lines, w_inner, w_outer).reshape(member.shape)


def plane_fn(plane, w_row, w_col):
    after_rows = sublayer(plane[None], *w_row)[0]
    return sublayer(after_rows[:, :, None, :], *w_col)[:, :, 0, :]


def to_planes(depth_lines, sizes):
    nz, ny, nx = sizes
    z_len, yl, kx, feat = depth_lines.shape
    got = lax.all_to_all(depth_lines, ALL, 0, 0, tiled=True)
    got = got.reshape(nz, ny, nx, yl, kx, feat)
    return jnp.transpose(got, (1, 3, 2, 0, 4, 5)).reshape(ny * yl, nx * nz * kx, feat)


def from_planes(plane, sizes):
    nz, ny, nx = sizes
    rows, cols, feat = plane.shape
    yl, kx = rows // ny, cols // (nx * nz)
    parts = plane.reshape(ny, yl, nx, nz, kx, feat)
    parts = jnp.transpose(parts, (3, 0, 2, 1, 4, 5)).reshape(nz * ny * nx, yl, kx, feat)
    return lax.all_to_all(parts, ALL, 0, 0, tiled=True)


def block_to_plane(block, sizes):
    nz, ny, nx = sizes
    zl, yl, xl, feat = block.shape
    got = lax.all_to_all(block, ("gy", "gx"), 0, 0, tiled=True)
    got = got.reshape(ny, nx, yl, xl, feat)
    return jnp.transpose(got, (0, 2, 1, 3, 4)).reshape(ny * yl, nx * xl, feat)


def local(volume, cotangent, w_project, w_output, sizes):
    w_depth, w_row, w_col = full_weights(w_project, w_output, sizes)

    depth_act = lax.all_to_all(volume, "gz", 2, 0, tiled=True)
    cot_plane = block_to_plane(cotangent, sizes)

    field_one, depth_pullback = jax.vjp(lambda m: depth_fn(m, *w_depth), depth_act)
    plane_one = to_planes(field_one, sizes)
    _, plane_pullback = jax.vjp(lambda p: plane_fn(p, w_row, w_col), plane_one)
    grad_plane = plane_pullback(cot_plane)[0]
    grad_one = from_planes(grad_plane, sizes)
    grad_zero = depth_pullback(grad_one)[0]
    return lax.all_to_all(grad_zero, "gz", 0, 2, tiled=True)


def along_rows(member, w_inner, w_outer):
    return sublayer(member, w_inner, w_outer)


def along_columns(member, w_inner, w_outer):
    depth_len, row_len, col_len, feat_len = member.shape
    flat_lines = member.reshape(depth_len * row_len, col_len, 1, feat_len)
    return sublayer(flat_lines, w_inner, w_outer).reshape(member.shape)


def line_swap(stacked, axis, split_axis, concat_axis):
    return lax.all_to_all(stacked, axis, split_axis=split_axis, concat_axis=concat_axis, tiled=True)


def local_general(volume, cotangent, w_project, w_output, sizes):
    w_depth, w_row, w_col = full_weights(w_project, w_output, sizes)

    def row_fn(member):
        return along_rows(member, *w_row)

    def column_fn(member):
        return along_columns(member, *w_col)

    depth_act = line_swap(volume, "gz", 2, 0)
    field_one, depth_pullback = jax.vjp(lambda m: depth_fn(m, *w_depth), depth_act)
    field_one = line_swap(field_one, "gz", 0, 2)
    row_act = line_swap(field_one, "gy", 2, 1)
    field_two, row_pullback = jax.vjp(row_fn, row_act)
    field_two = line_swap(field_two, "gy", 1, 2)
    paired = line_swap(jnp.stack([cotangent, field_two]), "gx", 1, 3)
    _, column_pullback = jax.vjp(column_fn, paired[1])
    grad_two = line_swap(column_pullback(paired[0])[0], "gx", 2, 0)
    grad_one = line_swap(row_pullback(line_swap(grad_two, "gy", 2, 1))[0], "gy", 1, 2)
    grad_zero = depth_pullback(line_swap(grad_one, "gz", 2, 0))[0]
    return line_swap(grad_zero, "gz", 0, 2)


def solution(mesh):
    sizes = (mesh.shape["gz"], mesh.shape["gy"], mesh.shape["gx"])

    def body(volume, *rest):
        one_depth = volume.shape[0] * sizes[0] == mesh.size
        return (local if one_depth else local_general)(volume, *rest, sizes)

    return jax.shard_map(
        body,
        mesh=mesh,
        in_specs=(
            P("gz", "gy", "gx", None),
            P("gz", "gy", "gx", None),
            P(None, "gy", ("gz", "gx")),
            P(None, "gy", ("gz", "gx")),
        ),
        out_specs=P("gz", "gy", "gx", None),
        check_vma=False,
    )
```

```python
import jax
import jax.numpy as jnp
from jax import lax
from jax.sharding import PartitionSpec as P

HEADS = 6
HIGHEST = lax.Precision.HIGHEST
ALL = ("gz", "gy", "gx")


def head_map(feat_len):
    head_size = feat_len // HEADS
    return (jnp.arange(feat_len)[:, None] // head_size == jnp.arange(HEADS)[None, :]).astype(jnp.float32)


def head_norm(vector, ones):
    head_size = vector.shape[-1] // HEADS
    sums = jnp.dot(vector * vector, ones, precision=HIGHEST)
    scale = lax.rsqrt(sums / head_size + 1e-06)
    return (vector * jnp.dot(scale, ones.T, precision=HIGHEST)).astype(jnp.bfloat16)


def sublayer(line_rows, w_inner, w_outer):
    feat_len = line_rows.shape[-1]
    head_size = feat_len // HEADS
    ones = head_map(feat_len)
    mask = ones.T.astype(jnp.bfloat16)
    stream = line_rows.astype(jnp.float32)
    normed = (stream * lax.rsqrt(jnp.mean(stream * stream, axis=-1, keepdims=True) + 1e-06)).astype(jnp.bfloat16)
    packed = jnp.dot(normed, w_inner, preferred_element_type=jnp.float32)
    queries = head_norm(packed[..., :feat_len], ones)
    key_part = head_norm(packed[..., feat_len : 2 * feat_len], ones)
    value_part = packed[..., 2 * feat_len :].astype(jnp.bfloat16)
    key_heads = key_part[..., None, :] * mask
    scores = jnp.einsum("plqd,pkqhd->pqhlk", queries, key_heads, preferred_element_type=jnp.float32) * head_size ** (-0.5)
    powers = jnp.exp(scores)
    attn_weights = (powers / jnp.sum(powers, axis=-1, keepdims=True)).astype(jnp.bfloat16)
    mixed_heads = jnp.einsum("pqhlk,pkqd->plqhd", attn_weights, value_part, preferred_element_type=jnp.float32)
    mixed_out = jnp.sum(mixed_heads * mask.astype(jnp.float32), axis=-2).astype(jnp.bfloat16)
    update = jnp.dot(mixed_out, w_outer, preferred_element_type=jnp.float32)
    return (stream + update).astype(jnp.bfloat16)


def full_weights(w_project, w_output, sizes):
    subs, din, dproj = w_project.shape
    cat = jnp.concatenate([w_project, w_output], axis=2)
    ny = sizes[1]
    shifted = [cat] + [
        lax.ppermute(cat, "gy", [(i, (i + s) % ny) for i in range(ny)]) for s in range(1, ny)
    ]
    source = (lax.axis_index("gy") - jnp.arange(ny)) % ny
    rows = jnp.take(jnp.stack(shifted), source, axis=0)
    rows = jnp.swapaxes(rows, 0, 1).reshape(subs, ny * din, cat.shape[2])
    proj = lax.all_gather(rows[:, :, :dproj], ("gz", "gx"), axis=2, tiled=True)
    outp = lax.all_gather(rows[:, :, dproj:], ("gz", "gx"), axis=2, tiled=True)
    return [(proj[i], outp[i]) for i in range(subs)]


def depth_fn(member, w_inner, w_outer):
    depth_len, row_len, rest_len, feat_len = member.shape
    flat_lines = member.reshape(1, depth_len, row_len * rest_len, feat_len)
    return sublayer(flat_lines, w_inner, w_outer).reshape(member.shape)


def plane_fn(plane, w_row, w_col):
    after_rows = sublayer(plane[None], *w_row)[0]
    return sublayer(after_rows[:, :, None, :], *w_col)[:, :, 0, :]


def to_planes(depth_lines, sizes):
    nz, ny, nx = sizes
    z_len, yl, kx, feat = depth_lines.shape
    got = lax.all_to_all(depth_lines, ALL, 0, 0, tiled=True)
    got = got.reshape(nz, ny, nx, yl, kx, feat)
    return jnp.transpose(got, (1, 3, 2, 0, 4, 5)).reshape(ny * yl, nx * nz * kx, feat)


def from_planes(plane, sizes):
    nz, ny, nx = sizes
    rows, cols, feat = plane.shape
    yl, kx = rows // ny, cols // (nx * nz)
    parts = plane.reshape(ny, yl, nx, nz, kx, feat)
    parts = jnp.transpose(parts, (3, 0, 2, 1, 4, 5)).reshape(nz * ny * nx, yl, kx, feat)
    return lax.all_to_all(parts, ALL, 0, 0, tiled=True)


def block_to_plane(block, sizes):
    nz, ny, nx = sizes
    zl, yl, xl, feat = block.shape
    got = lax.all_to_all(block, ("gy", "gx"), 0, 0, tiled=True)
    got = got.reshape(ny, nx, yl, xl, feat)
    return jnp.transpose(got, (0, 2, 1, 3, 4)).reshape(ny * yl, nx * xl, feat)


def local(volume, cotangent, w_project, w_output, sizes):
    w_depth, w_row, w_col = full_weights(w_project, w_output, sizes)

    depth_act = lax.all_to_all(volume, "gz", 2, 0, tiled=True)
    cot_plane = block_to_plane(cotangent, sizes)

    field_one, depth_pullback = jax.vjp(lambda m: depth_fn(m, *w_depth), depth_act)
    plane_one = to_planes(field_one, sizes)
    _, plane_pullback = jax.vjp(lambda p: plane_fn(p, w_row, w_col), plane_one)
    grad_plane = plane_pullback(cot_plane)[0]
    grad_one = from_planes(grad_plane, sizes)
    grad_zero = depth_pullback(grad_one)[0]
    return lax.all_to_all(grad_zero, "gz", 0, 2, tiled=True)


def along_rows(member, w_inner, w_outer):
    return sublayer(member, w_inner, w_outer)


def along_columns(member, w_inner, w_outer):
    depth_len, row_len, col_len, feat_len = member.shape
    flat_lines = member.reshape(depth_len * row_len, col_len, 1, feat_len)
    return sublayer(flat_lines, w_inner, w_outer).reshape(member.shape)


def line_swap(stacked, axis, split_axis, concat_axis):
    return lax.all_to_all(stacked, axis, split_axis=split_axis, concat_axis=concat_axis, tiled=True)


def local_general(volume, cotangent, w_project, w_output, sizes):
    w_depth, w_row, w_col = full_weights(w_project, w_output, sizes)

    def row_fn(member):
        return along_rows(member, *w_row)

    def column_fn(member):
        return along_columns(member, *w_col)

    depth_act = line_swap(volume, "gz", 2, 0)
    field_one, depth_pullback = jax.vjp(lambda m: depth_fn(m, *w_depth), depth_act)
    field_one = line_swap(field_one, "gz", 0, 2)
    row_act = line_swap(field_one, "gy", 2, 1)
    field_two, row_pullback = jax.vjp(row_fn, row_act)
    field_two = line_swap(field_two, "gy", 1, 2)
    paired = line_swap(jnp.stack([cotangent, field_two]), "gx", 1, 3)
    _, column_pullback = jax.vjp(column_fn, paired[1])
    grad_two = line_swap(column_pullback(paired[0])[0], "gx", 2, 0)
    grad_one = line_swap(row_pullback(line_swap(grad_two, "gy", 2, 1))[0], "gy", 1, 2)
    grad_zero = depth_pullback(line_swap(grad_one, "gz", 2, 0))[0]
    return line_swap(grad_zero, "gz", 0, 2)


def solution(mesh):
    sizes = (mesh.shape["gz"], mesh.shape["gy"], mesh.shape["gx"])

    def body(volume, *rest):
        one_depth = volume.shape[0] * sizes[0] == mesh.size
        return (local if one_depth else local_general)(volume, *rest, sizes)

    return jax.shard_map(
        body,
        mesh=mesh,
        in_specs=(
            P("gz", "gy", "gx", None),
            P("gz", "gy", "gx", None),
            P(None, "gy", ("gz", "gx")),
            P(None, "gy", ("gz", "gx")),
        ),
        out_specs=P("gz", "gy", "gx", None),
        check_vma=False,
    )
```

```python
import jax
import jax.numpy as jnp
from jax import lax
from jax.sharding import PartitionSpec as P

HEADS = 6
HIGHEST = lax.Precision.HIGHEST
ALL = ("gz", "gy", "gx")


def head_map(feat_len):
    head_size = feat_len // HEADS
    return (jnp.arange(feat_len)[:, None] // head_size == jnp.arange(HEADS)[None, :]).astype(jnp.float32)


def head_norm(vector, ones):
    head_size = vector.shape[-1] // HEADS
    sums = jnp.dot(vector * vector, ones, precision=HIGHEST)
    scale = lax.rsqrt(sums / head_size + 1e-06)
    return (vector * jnp.dot(scale, ones.T, precision=HIGHEST)).astype(jnp.bfloat16)


def sublayer(line_rows, w_inner, w_outer):
    feat_len = line_rows.shape[-1]
    head_size = feat_len // HEADS
    ones = head_map(feat_len)
    mask = ones.T.astype(jnp.bfloat16)
    stream = line_rows.astype(jnp.float32)
    normed = (stream * lax.rsqrt(jnp.mean(stream * stream, axis=-1, keepdims=True) + 1e-06)).astype(jnp.bfloat16)
    packed = jnp.dot(normed, w_inner, preferred_element_type=jnp.float32)
    queries = head_norm(packed[..., :feat_len], ones)
    key_part = head_norm(packed[..., feat_len : 2 * feat_len], ones)
    value_part = packed[..., 2 * feat_len :].astype(jnp.bfloat16)
    key_heads = key_part[..., None, :] * mask
    scores = jnp.einsum("plqd,pkqhd->pqhlk", queries, key_heads, preferred_element_type=jnp.float32) * head_size ** (-0.5)
    powers = jnp.exp(scores)
    attn_weights = (powers / jnp.sum(powers, axis=-1, keepdims=True)).astype(jnp.bfloat16)
    mixed_heads = jnp.einsum("pqhlk,pkqd->plqhd", attn_weights, value_part, preferred_element_type=jnp.float32)
    mixed_out = jnp.sum(mixed_heads * mask.astype(jnp.float32), axis=-2).astype(jnp.bfloat16)
    update = jnp.dot(mixed_out, w_outer, preferred_element_type=jnp.float32)
    return (stream + update).astype(jnp.bfloat16)


def full_weights(w_project, w_output, sizes):
    subs, din, dproj = w_project.shape
    cat = jnp.concatenate([w_project, w_output], axis=2)
    ny = sizes[1]
    shifted = [cat] + [
        lax.ppermute(cat, "gy", [(i, (i + s) % ny) for i in range(ny)]) for s in range(1, ny)
    ]
    source = (lax.axis_index("gy") - jnp.arange(ny)) % ny
    rows = jnp.take(jnp.stack(shifted), source, axis=0)
    rows = jnp.swapaxes(rows, 0, 1).reshape(subs, ny * din, cat.shape[2])
    feat = rows.shape[1]
    blocks = sizes[0] * sizes[2]
    dout = w_output.shape[2]
    outp = rows[:, :, dproj:].reshape(subs, -1, dproj)
    got = lax.all_gather(
        jnp.concatenate([rows[:, :, :dproj], outp], axis=1), ("gz", "gx"), axis=2, tiled=True
    )
    proj = got[:, :feat]
    outp = got[:, feat:].reshape(subs, -1, blocks, dproj).swapaxes(1, 2)
    outp = outp.reshape(subs, blocks, feat, dout).swapaxes(1, 2).reshape(subs, feat, blocks * dout)
    return [(proj[i], outp[i]) for i in range(subs)]


def depth_fn(member, w_inner, w_outer):
    depth_len, row_len, rest_len, feat_len = member.shape
    flat_lines = member.reshape(1, depth_len, row_len * rest_len, feat_len)
    return sublayer(flat_lines, w_inner, w_outer).reshape(member.shape)


def plane_fn(plane, w_row, w_col):
    after_rows = sublayer(plane[None], *w_row)[0]
    return sublayer(after_rows[:, :, None, :], *w_col)[:, :, 0, :]


def to_planes(depth_lines, sizes):
    nz, ny, nx = sizes
    z_len, yl, kx, feat = depth_lines.shape
    got = lax.all_to_all(depth_lines, ALL, 0, 0, tiled=True)
    got = got.reshape(nz, ny, nx, yl, kx, feat)
    return jnp.transpose(got, (1, 3, 2, 0, 4, 5)).reshape(ny * yl, nx * nz * kx, feat)


def from_planes(plane, sizes):
    nz, ny, nx = sizes
    rows, cols, feat = plane.shape
    yl, kx = rows // ny, cols // (nx * nz)
    parts = plane.reshape(ny, yl, nx, nz, kx, feat)
    parts = jnp.transpose(parts, (3, 0, 2, 1, 4, 5)).reshape(nz * ny * nx, yl, kx, feat)
    return lax.all_to_all(parts, ALL, 0, 0, tiled=True)


def block_to_plane(block, sizes):
    nz, ny, nx = sizes
    zl, yl, xl, feat = block.shape
    got = lax.all_to_all(block, ("gy", "gx"), 0, 0, tiled=True)
    got = got.reshape(ny, nx, yl, xl, feat)
    return jnp.transpose(got, (0, 2, 1, 3, 4)).reshape(ny * yl, nx * xl, feat)


def local(volume, cotangent, w_project, w_output, sizes):
    w_depth, w_row, w_col = full_weights(w_project, w_output, sizes)

    depth_act = lax.all_to_all(volume, "gz", 2, 0, tiled=True)
    cot_plane = block_to_plane(cotangent, sizes)

    field_one, depth_pullback = jax.vjp(lambda m: depth_fn(m, *w_depth), depth_act)
    plane_one = to_planes(field_one, sizes)
    _, plane_pullback = jax.vjp(lambda p: plane_fn(p, w_row, w_col), plane_one)
    grad_plane = plane_pullback(cot_plane)[0]
    grad_one = from_planes(grad_plane, sizes)
    grad_zero = depth_pullback(grad_one)[0]
    return lax.all_to_all(grad_zero, "gz", 0, 2, tiled=True)


def along_rows(member, w_inner, w_outer):
    return sublayer(member, w_inner, w_outer)


def along_columns(member, w_inner, w_outer):
    depth_len, row_len, col_len, feat_len = member.shape
    flat_lines = member.reshape(depth_len * row_len, col_len, 1, feat_len)
    return sublayer(flat_lines, w_inner, w_outer).reshape(member.shape)


def line_swap(stacked, axis, split_axis, concat_axis):
    return lax.all_to_all(stacked, axis, split_axis=split_axis, concat_axis=concat_axis, tiled=True)


def local_general(volume, cotangent, w_project, w_output, sizes):
    w_depth, w_row, w_col = full_weights(w_project, w_output, sizes)

    def row_fn(member):
        return along_rows(member, *w_row)

    def column_fn(member):
        return along_columns(member, *w_col)

    depth_act = line_swap(volume, "gz", 2, 0)
    field_one, depth_pullback = jax.vjp(lambda m: depth_fn(m, *w_depth), depth_act)
    field_one = line_swap(field_one, "gz", 0, 2)
    row_act = line_swap(field_one, "gy", 2, 1)
    field_two, row_pullback = jax.vjp(row_fn, row_act)
    field_two = line_swap(field_two, "gy", 1, 2)
    paired = line_swap(jnp.stack([cotangent, field_two]), "gx", 1, 3)
    _, column_pullback = jax.vjp(column_fn, paired[1])
    grad_two = line_swap(column_pullback(paired[0])[0], "gx", 2, 0)
    grad_one = line_swap(row_pullback(line_swap(grad_two, "gy", 2, 1))[0], "gy", 1, 2)
    grad_zero = depth_pullback(line_swap(grad_one, "gz", 2, 0))[0]
    return line_swap(grad_zero, "gz", 0, 2)


def solution(mesh):
    sizes = (mesh.shape["gz"], mesh.shape["gy"], mesh.shape["gx"])

    def body(volume, *rest):
        one_depth = volume.shape[0] * sizes[0] == mesh.size
        return (local if one_depth else local_general)(volume, *rest, sizes)

    return jax.shard_map(
        body,
        mesh=mesh,
        in_specs=(
            P("gz", "gy", "gx", None),
            P("gz", "gy", "gx", None),
            P(None, "gy", ("gz", "gx")),
            P(None, "gy", ("gz", "gx")),
        ),
        out_specs=P("gz", "gy", "gx", None),
        check_vma=False,
    )
```

```python
import jax
import jax.numpy as jnp
from jax import lax
from jax.sharding import PartitionSpec as P

HEADS = 6
HIGHEST = lax.Precision.HIGHEST
ALL = ("gz", "gy", "gx")


def head_map(feat_len):
    head_size = feat_len // HEADS
    return (jnp.arange(feat_len)[:, None] // head_size == jnp.arange(HEADS)[None, :]).astype(jnp.float32)


def head_norm(vector, ones):
    head_size = vector.shape[-1] // HEADS
    sums = jnp.dot(vector * vector, ones, precision=HIGHEST)
    scale = lax.rsqrt(sums / head_size + 1e-06)
    return (vector * jnp.dot(scale, ones.T, precision=HIGHEST)).astype(jnp.bfloat16)


def sublayer(line_rows, w_inner, w_outer):
    feat_len = line_rows.shape[-1]
    head_size = feat_len // HEADS
    ones = head_map(feat_len)
    mask = ones.T.astype(jnp.bfloat16)
    stream = line_rows.astype(jnp.float32)
    normed = (stream * lax.rsqrt(jnp.mean(stream * stream, axis=-1, keepdims=True) + 1e-06)).astype(jnp.bfloat16)
    packed = jnp.dot(normed, w_inner, preferred_element_type=jnp.float32)
    queries = head_norm(packed[..., :feat_len], ones)
    key_part = head_norm(packed[..., feat_len : 2 * feat_len], ones)
    value_part = packed[..., 2 * feat_len :].astype(jnp.bfloat16)
    key_heads = key_part[..., None, :] * mask
    scores = jnp.einsum("plqd,pkqhd->pqhlk", queries, key_heads, preferred_element_type=jnp.float32) * head_size ** (-0.5)
    powers = jnp.exp(scores)
    attn_weights = (powers / jnp.sum(powers, axis=-1, keepdims=True)).astype(jnp.bfloat16)
    mixed_heads = jnp.einsum("pqhlk,pkqd->plqhd", attn_weights, value_part, preferred_element_type=jnp.float32)
    mixed_out = jnp.sum(mixed_heads * mask.astype(jnp.float32), axis=-2).astype(jnp.bfloat16)
    update = jnp.dot(mixed_out, w_outer, preferred_element_type=jnp.float32)
    return (stream + update).astype(jnp.bfloat16)


def full_weights(w_project, w_output, sizes):
    subs, din, dproj = w_project.shape
    cat = jnp.concatenate([w_project, w_output], axis=2)
    ny = sizes[1]
    shifted = [cat] + [
        lax.ppermute(cat, "gy", [(i, (i + s) % ny) for i in range(ny)]) for s in range(1, ny)
    ]
    source = (lax.axis_index("gy") - jnp.arange(ny)) % ny
    rows = jnp.take(jnp.stack(shifted), source, axis=0)
    rows = jnp.swapaxes(rows, 0, 1).reshape(subs, ny * din, cat.shape[2])
    feat = rows.shape[1]
    blocks = sizes[0] * sizes[2]
    dout = w_output.shape[2]
    weights = []
    for part in (rows[:1], rows[1:]):
        count = part.shape[0]
        stacked = jnp.concatenate([part[:, :, :dproj], part[:, :, dproj:].reshape(count, -1, dproj)], axis=1)
        got = lax.all_gather(stacked, ("gz", "gx"), axis=2, tiled=True)
        outp = got[:, feat:].reshape(count, -1, blocks, dproj).swapaxes(1, 2)
        outp = outp.reshape(count, blocks, feat, dout).swapaxes(1, 2).reshape(count, feat, blocks * dout)
        weights += [(got[i, :feat], outp[i]) for i in range(count)]
    return weights


def depth_fn(member, w_inner, w_outer):
    depth_len, row_len, rest_len, feat_len = member.shape
    flat_lines = member.reshape(1, depth_len, row_len * rest_len, feat_len)
    return sublayer(flat_lines, w_inner, w_outer).reshape(member.shape)


def plane_fn(plane, w_row, w_col):
    after_rows = sublayer(plane[None], *w_row)[0]
    return sublayer(after_rows[:, :, None, :], *w_col)[:, :, 0, :]


def to_planes(depth_lines, sizes):
    nz, ny, nx = sizes
    z_len, yl, kx, feat = depth_lines.shape
    got = lax.all_to_all(depth_lines, ALL, 0, 0, tiled=True)
    got = got.reshape(nz, ny, nx, yl, kx, feat)
    return jnp.transpose(got, (1, 3, 2, 0, 4, 5)).reshape(ny * yl, nx * nz * kx, feat)


def from_planes(plane, sizes):
    nz, ny, nx = sizes
    rows, cols, feat = plane.shape
    yl, kx = rows // ny, cols // (nx * nz)
    parts = plane.reshape(ny, yl, nx, nz, kx, feat)
    parts = jnp.transpose(parts, (3, 0, 2, 1, 4, 5)).reshape(nz * ny * nx, yl, kx, feat)
    return lax.all_to_all(parts, ALL, 0, 0, tiled=True)


def block_to_plane(block, sizes):
    nz, ny, nx = sizes
    zl, yl, xl, feat = block.shape
    got = lax.all_to_all(block, ("gy", "gx"), 0, 0, tiled=True)
    got = got.reshape(ny, nx, yl, xl, feat)
    return jnp.transpose(got, (0, 2, 1, 3, 4)).reshape(ny * yl, nx * xl, feat)


def local(volume, cotangent, w_project, w_output, sizes):
    w_depth, w_row, w_col = full_weights(w_project, w_output, sizes)

    depth_act = lax.all_to_all(volume, "gz", 2, 0, tiled=True)
    cot_plane = block_to_plane(cotangent, sizes)

    field_one, depth_pullback = jax.vjp(lambda m: depth_fn(m, *w_depth), depth_act)
    plane_one = to_planes(field_one, sizes)
    _, plane_pullback = jax.vjp(lambda p: plane_fn(p, w_row, w_col), plane_one)
    grad_plane = plane_pullback(cot_plane)[0]
    grad_one = from_planes(grad_plane, sizes)
    grad_zero = depth_pullback(grad_one)[0]
    return lax.all_to_all(grad_zero, "gz", 0, 2, tiled=True)


def along_rows(member, w_inner, w_outer):
    return sublayer(member, w_inner, w_outer)


def along_columns(member, w_inner, w_outer):
    depth_len, row_len, col_len, feat_len = member.shape
    flat_lines = member.reshape(depth_len * row_len, col_len, 1, feat_len)
    return sublayer(flat_lines, w_inner, w_outer).reshape(member.shape)


def line_swap(stacked, axis, split_axis, concat_axis):
    return lax.all_to_all(stacked, axis, split_axis=split_axis, concat_axis=concat_axis, tiled=True)


def local_general(volume, cotangent, w_project, w_output, sizes):
    w_depth, w_row, w_col = full_weights(w_project, w_output, sizes)

    def row_fn(member):
        return along_rows(member, *w_row)

    def column_fn(member):
        return along_columns(member, *w_col)

    depth_act = line_swap(volume, "gz", 2, 0)
    field_one, depth_pullback = jax.vjp(lambda m: depth_fn(m, *w_depth), depth_act)
    field_one = line_swap(field_one, "gz", 0, 2)
    row_act = line_swap(field_one, "gy", 2, 1)
    field_two, row_pullback = jax.vjp(row_fn, row_act)
    field_two = line_swap(field_two, "gy", 1, 2)
    paired = line_swap(jnp.stack([cotangent, field_two]), "gx", 1, 3)
    _, column_pullback = jax.vjp(column_fn, paired[1])
    grad_two = line_swap(column_pullback(paired[0])[0], "gx", 2, 0)
    grad_one = line_swap(row_pullback(line_swap(grad_two, "gy", 2, 1))[0], "gy", 1, 2)
    grad_zero = depth_pullback(line_swap(grad_one, "gz", 2, 0))[0]
    return line_swap(grad_zero, "gz", 0, 2)


def solution(mesh):
    sizes = (mesh.shape["gz"], mesh.shape["gy"], mesh.shape["gx"])

    def body(volume, *rest):
        one_depth = volume.shape[0] * sizes[0] == mesh.size
        return (local if one_depth else local_general)(volume, *rest, sizes)

    return jax.shard_map(
        body,
        mesh=mesh,
        in_specs=(
            P("gz", "gy", "gx", None),
            P("gz", "gy", "gx", None),
            P(None, "gy", ("gz", "gx")),
            P(None, "gy", ("gz", "gx")),
        ),
        out_specs=P("gz", "gy", "gx", None),
        check_vma=False,
    )
```

```python
import jax
import jax.numpy as jnp
from jax import lax
from jax.sharding import PartitionSpec as P

HEADS = 6
HIGHEST = lax.Precision.HIGHEST
ALL = ("gz", "gy", "gx")


def head_map(feat_len):
    head_size = feat_len // HEADS
    return (jnp.arange(feat_len)[:, None] // head_size == jnp.arange(HEADS)[None, :]).astype(jnp.float32)


def head_norm(vector, ones):
    head_size = vector.shape[-1] // HEADS
    sums = jnp.dot(vector * vector, ones, precision=HIGHEST)
    scale = lax.rsqrt(sums / head_size + 1e-06)
    return (vector * jnp.dot(scale, ones.T, precision=HIGHEST)).astype(jnp.bfloat16)


def sublayer(line_rows, w_inner, w_outer):
    feat_len = line_rows.shape[-1]
    head_size = feat_len // HEADS
    ones = head_map(feat_len)
    mask = ones.T.astype(jnp.bfloat16)
    stream = line_rows.astype(jnp.float32)
    normed = (stream * lax.rsqrt(jnp.mean(stream * stream, axis=-1, keepdims=True) + 1e-06)).astype(jnp.bfloat16)
    packed = jnp.dot(normed, w_inner, preferred_element_type=jnp.float32)
    queries = head_norm(packed[..., :feat_len], ones)
    key_part = head_norm(packed[..., feat_len : 2 * feat_len], ones)
    value_part = packed[..., 2 * feat_len :].astype(jnp.bfloat16)
    key_heads = key_part[..., None, :] * mask
    scores = jnp.einsum("plqd,pkqhd->pqhlk", queries, key_heads, preferred_element_type=jnp.float32) * head_size ** (-0.5)
    powers = jnp.exp(scores)
    attn_weights = (powers / jnp.sum(powers, axis=-1, keepdims=True)).astype(jnp.bfloat16)
    mixed_heads = jnp.einsum("pqhlk,pkqd->plqhd", attn_weights, value_part, preferred_element_type=jnp.float32)
    mixed_out = jnp.sum(mixed_heads * mask.astype(jnp.float32), axis=-2).astype(jnp.bfloat16)
    update = jnp.dot(mixed_out, w_outer, preferred_element_type=jnp.float32)
    return (stream + update).astype(jnp.bfloat16)


def full_weights(w_project, w_output, sizes):
    subs, din, dproj = w_project.shape
    nz, ny, nx = sizes
    shifted = [w_project] + [
        lax.ppermute(w_project, "gy", [(i, (i + s) % ny) for i in range(ny)]) for s in range(1, ny)
    ]
    source = (lax.axis_index("gy") - jnp.arange(ny)) % ny
    rows = jnp.take(jnp.stack(shifted), source, axis=0)
    rows = jnp.swapaxes(rows, 0, 1).reshape(subs, ny * din, dproj)
    proj = lax.all_gather(rows, ("gz", "gx"), axis=2, tiled=True)
    outp = lax.all_gather(w_output, ALL, axis=0, tiled=False)
    outp = outp.reshape((nz, ny, nx) + w_output.shape)
    outp = jnp.transpose(outp, (3, 1, 4, 0, 2, 5)).reshape(subs, ny * din, -1)
    return [(proj[i], outp[i]) for i in range(subs)]


def depth_fn(member, w_inner, w_outer):
    depth_len, row_len, rest_len, feat_len = member.shape
    flat_lines = member.reshape(1, depth_len, row_len * rest_len, feat_len)
    return sublayer(flat_lines, w_inner, w_outer).reshape(member.shape)


def plane_fn(plane, w_row, w_col):
    after_rows = sublayer(plane[None], *w_row)[0]
    return sublayer(after_rows[:, :, None, :], *w_col)[:, :, 0, :]


def to_planes(depth_lines, sizes):
    nz, ny, nx = sizes
    z_len, yl, kx, feat = depth_lines.shape
    got = lax.all_to_all(depth_lines, ALL, 0, 0, tiled=True)
    got = got.reshape(nz, ny, nx, yl, kx, feat)
    return jnp.transpose(got, (1, 3, 2, 0, 4, 5)).reshape(ny * yl, nx * nz * kx, feat)


def from_planes(plane, sizes):
    nz, ny, nx = sizes
    rows, cols, feat = plane.shape
    yl, kx = rows // ny, cols // (nx * nz)
    parts = plane.reshape(ny, yl, nx, nz, kx, feat)
    parts = jnp.transpose(parts, (3, 0, 2, 1, 4, 5)).reshape(nz * ny * nx, yl, kx, feat)
    return lax.all_to_all(parts, ALL, 0, 0, tiled=True)


def block_to_plane(block, sizes):
    nz, ny, nx = sizes
    zl, yl, xl, feat = block.shape
    got = lax.all_to_all(block, ("gy", "gx"), 0, 0, tiled=True)
    got = got.reshape(ny, nx, yl, xl, feat)
    return jnp.transpose(got, (0, 2, 1, 3, 4)).reshape(ny * yl, nx * xl, feat)


def local(volume, cotangent, w_project, w_output, sizes):
    w_depth, w_row, w_col = full_weights(w_project, w_output, sizes)

    depth_act = lax.all_to_all(volume, "gz", 2, 0, tiled=True)
    cot_plane = block_to_plane(cotangent, sizes)

    field_one, depth_pullback = jax.vjp(lambda m: depth_fn(m, *w_depth), depth_act)
    plane_one = to_planes(field_one, sizes)
    _, plane_pullback = jax.vjp(lambda p: plane_fn(p, w_row, w_col), plane_one)
    grad_plane = plane_pullback(cot_plane)[0]
    grad_one = from_planes(grad_plane, sizes)
    grad_zero = depth_pullback(grad_one)[0]
    return lax.all_to_all(grad_zero, "gz", 0, 2, tiled=True)


def along_rows(member, w_inner, w_outer):
    return sublayer(member, w_inner, w_outer)


def along_columns(member, w_inner, w_outer):
    depth_len, row_len, col_len, feat_len = member.shape
    flat_lines = member.reshape(depth_len * row_len, col_len, 1, feat_len)
    return sublayer(flat_lines, w_inner, w_outer).reshape(member.shape)


def line_swap(stacked, axis, split_axis, concat_axis):
    return lax.all_to_all(stacked, axis, split_axis=split_axis, concat_axis=concat_axis, tiled=True)


def local_general(volume, cotangent, w_project, w_output, sizes):
    w_depth, w_row, w_col = full_weights(w_project, w_output, sizes)

    def row_fn(member):
        return along_rows(member, *w_row)

    def column_fn(member):
        return along_columns(member, *w_col)

    depth_act = line_swap(volume, "gz", 2, 0)
    field_one, depth_pullback = jax.vjp(lambda m: depth_fn(m, *w_depth), depth_act)
    field_one = line_swap(field_one, "gz", 0, 2)
    row_act = line_swap(field_one, "gy", 2, 1)
    field_two, row_pullback = jax.vjp(row_fn, row_act)
    field_two = line_swap(field_two, "gy", 1, 2)
    paired = line_swap(jnp.stack([cotangent, field_two]), "gx", 1, 3)
    _, column_pullback = jax.vjp(column_fn, paired[1])
    grad_two = line_swap(column_pullback(paired[0])[0], "gx", 2, 0)
    grad_one = line_swap(row_pullback(line_swap(grad_two, "gy", 2, 1))[0], "gy", 1, 2)
    grad_zero = depth_pullback(line_swap(grad_one, "gz", 2, 0))[0]
    return line_swap(grad_zero, "gz", 0, 2)


def solution(mesh):
    sizes = (mesh.shape["gz"], mesh.shape["gy"], mesh.shape["gx"])

    def body(volume, *rest):
        one_depth = volume.shape[0] * sizes[0] == mesh.size
        return (local if one_depth else local_general)(volume, *rest, sizes)

    return jax.shard_map(
        body,
        mesh=mesh,
        in_specs=(
            P("gz", "gy", "gx", None),
            P("gz", "gy", "gx", None),
            P(None, "gy", ("gz", "gx")),
            P(None, "gy", ("gz", "gx")),
        ),
        out_specs=P("gz", "gy", "gx", None),
        check_vma=False,
    )
```

```python
import jax
import jax.numpy as jnp
from jax import lax
from jax.sharding import PartitionSpec as P

HEADS = 6
HIGHEST = lax.Precision.HIGHEST
ALL = ("gz", "gy", "gx")


def head_map(feat_len):
    head_size = feat_len // HEADS
    return (jnp.arange(feat_len)[:, None] // head_size == jnp.arange(HEADS)[None, :]).astype(jnp.float32)


def head_norm(vector, ones):
    head_size = vector.shape[-1] // HEADS
    sums = jnp.dot(vector * vector, ones, precision=HIGHEST)
    scale = lax.rsqrt(sums / head_size + 1e-06)
    return (vector * jnp.dot(scale, ones.T, precision=HIGHEST)).astype(jnp.bfloat16)


def sublayer(line_rows, w_inner, w_outer):
    feat_len = line_rows.shape[-1]
    head_size = feat_len // HEADS
    ones = head_map(feat_len)
    mask = ones.T.astype(jnp.bfloat16)
    stream = line_rows.astype(jnp.float32)
    normed = (stream * lax.rsqrt(jnp.mean(stream * stream, axis=-1, keepdims=True) + 1e-06)).astype(jnp.bfloat16)
    packed = jnp.dot(normed, w_inner, preferred_element_type=jnp.float32)
    queries = head_norm(packed[..., :feat_len], ones)
    key_part = head_norm(packed[..., feat_len : 2 * feat_len], ones)
    value_part = packed[..., 2 * feat_len :].astype(jnp.bfloat16)
    if line_rows.shape[1] <= 8:
        pairs = queries[:, :, None].astype(jnp.float32) * key_part[:, None].astype(jnp.float32)
        scores = jnp.dot(pairs, ones, precision=HIGHEST) * head_size ** (-0.5)
        powers = jnp.exp(scores)
        attn_weights = (powers / jnp.sum(powers, axis=2, keepdims=True)).astype(jnp.bfloat16)
        spread = jnp.dot(attn_weights, mask, preferred_element_type=jnp.float32)
        mixed_out = jnp.sum(spread * value_part[:, None].astype(jnp.float32), axis=2).astype(jnp.bfloat16)
    else:
        key_heads = key_part[..., None, :] * mask
        scores = jnp.einsum(
            "plqd,pkqhd->pqhlk", queries, key_heads, preferred_element_type=jnp.float32
        ) * head_size ** (-0.5)
        powers = jnp.exp(scores)
        attn_weights = (powers / jnp.sum(powers, axis=-1, keepdims=True)).astype(jnp.bfloat16)
        mixed_heads = jnp.einsum(
            "pqhlk,pkqd->plqhd", attn_weights, value_part, preferred_element_type=jnp.float32
        )
        mixed_out = jnp.sum(mixed_heads * mask.astype(jnp.float32), axis=-2).astype(jnp.bfloat16)
    update = jnp.dot(mixed_out, w_outer, preferred_element_type=jnp.float32)
    return (stream + update).astype(jnp.bfloat16)


def full_weights(w_project, w_output, sizes):
    subs, din, dproj = w_project.shape
    cat = jnp.concatenate([w_project, w_output], axis=2)
    ny = sizes[1]
    shifted = [cat] + [
        lax.ppermute(cat, "gy", [(i, (i + s) % ny) for i in range(ny)]) for s in range(1, ny)
    ]
    source = (lax.axis_index("gy") - jnp.arange(ny)) % ny
    rows = jnp.take(jnp.stack(shifted), source, axis=0)
    rows = jnp.swapaxes(rows, 0, 1).reshape(subs, ny * din, cat.shape[2])
    proj = lax.all_gather(rows[:, :, :dproj], ("gz", "gx"), axis=2, tiled=True)
    outp = lax.all_gather(rows[:, :, dproj:], ("gz", "gx"), axis=2, tiled=True)
    return [(proj[i], outp[i]) for i in range(subs)]


def depth_fn(member, w_inner, w_outer):
    depth_len, row_len, rest_len, feat_len = member.shape
    flat_lines = member.reshape(1, depth_len, row_len * rest_len, feat_len)
    return sublayer(flat_lines, w_inner, w_outer).reshape(member.shape)


def plane_fn(plane, w_row, w_col):
    after_rows = sublayer(plane[None], *w_row)[0]
    return sublayer(after_rows[:, :, None, :], *w_col)[:, :, 0, :]


def to_planes(depth_lines, sizes):
    nz, ny, nx = sizes
    z_len, yl, kx, feat = depth_lines.shape
    got = lax.all_to_all(depth_lines, ALL, 0, 0, tiled=True)
    got = got.reshape(nz, ny, nx, yl, kx, feat)
    return jnp.transpose(got, (1, 3, 2, 0, 4, 5)).reshape(ny * yl, nx * nz * kx, feat)


def from_planes(plane, sizes):
    nz, ny, nx = sizes
    rows, cols, feat = plane.shape
    yl, kx = rows // ny, cols // (nx * nz)
    parts = plane.reshape(ny, yl, nx, nz, kx, feat)
    parts = jnp.transpose(parts, (3, 0, 2, 1, 4, 5)).reshape(nz * ny * nx, yl, kx, feat)
    return lax.all_to_all(parts, ALL, 0, 0, tiled=True)


def block_to_plane(block, sizes):
    nz, ny, nx = sizes
    zl, yl, xl, feat = block.shape
    got = lax.all_to_all(block, ("gy", "gx"), 0, 0, tiled=True)
    got = got.reshape(ny, nx, yl, xl, feat)
    return jnp.transpose(got, (0, 2, 1, 3, 4)).reshape(ny * yl, nx * xl, feat)


def local(volume, cotangent, w_project, w_output, sizes):
    w_depth, w_row, w_col = full_weights(w_project, w_output, sizes)

    depth_act = lax.all_to_all(volume, "gz", 2, 0, tiled=True)
    cot_plane = block_to_plane(cotangent, sizes)

    field_one, depth_pullback = jax.vjp(lambda m: depth_fn(m, *w_depth), depth_act)
    plane_one = to_planes(field_one, sizes)
    _, plane_pullback = jax.vjp(lambda p: plane_fn(p, w_row, w_col), plane_one)
    grad_plane = plane_pullback(cot_plane)[0]
    grad_one = from_planes(grad_plane, sizes)
    grad_zero = depth_pullback(grad_one)[0]
    return lax.all_to_all(grad_zero, "gz", 0, 2, tiled=True)


def along_rows(member, w_inner, w_outer):
    return sublayer(member, w_inner, w_outer)


def along_columns(member, w_inner, w_outer):
    depth_len, row_len, col_len, feat_len = member.shape
    flat_lines = member.reshape(depth_len * row_len, col_len, 1, feat_len)
    return sublayer(flat_lines, w_inner, w_outer).reshape(member.shape)


def line_swap(stacked, axis, split_axis, concat_axis):
    return lax.all_to_all(stacked, axis, split_axis=split_axis, concat_axis=concat_axis, tiled=True)


def local_general(volume, cotangent, w_project, w_output, sizes):
    w_depth, w_row, w_col = full_weights(w_project, w_output, sizes)

    def row_fn(member):
        return along_rows(member, *w_row)

    def column_fn(member):
        return along_columns(member, *w_col)

    depth_act = line_swap(volume, "gz", 2, 0)
    field_one, depth_pullback = jax.vjp(lambda m: depth_fn(m, *w_depth), depth_act)
    field_one = line_swap(field_one, "gz", 0, 2)
    row_act = line_swap(field_one, "gy", 2, 1)
    field_two, row_pullback = jax.vjp(row_fn, row_act)
    field_two = line_swap(field_two, "gy", 1, 2)
    paired = line_swap(jnp.stack([cotangent, field_two]), "gx", 1, 3)
    _, column_pullback = jax.vjp(column_fn, paired[1])
    grad_two = line_swap(column_pullback(paired[0])[0], "gx", 2, 0)
    grad_one = line_swap(row_pullback(line_swap(grad_two, "gy", 2, 1))[0], "gy", 1, 2)
    grad_zero = depth_pullback(line_swap(grad_one, "gz", 2, 0))[0]
    return line_swap(grad_zero, "gz", 0, 2)


def solution(mesh):
    sizes = (mesh.shape["gz"], mesh.shape["gy"], mesh.shape["gx"])

    def body(volume, *rest):
        one_depth = volume.shape[0] * sizes[0] == mesh.size
        return (local if one_depth else local_general)(volume, *rest, sizes)

    return jax.shard_map(
        body,
        mesh=mesh,
        in_specs=(
            P("gz", "gy", "gx", None),
            P("gz", "gy", "gx", None),
            P(None, "gy", ("gz", "gx")),
            P(None, "gy", ("gz", "gx")),
        ),
        out_specs=P("gz", "gy", "gx", None),
        check_vma=False,
    )
```

```python
import jax
import jax.numpy as jnp
from jax import lax
from jax.sharding import PartitionSpec as P

HEADS = 6
HIGHEST = lax.Precision.HIGHEST
ALL = ("gz", "gy", "gx")


def head_map(feat_len):
    head_size = feat_len // HEADS
    return (jnp.arange(feat_len)[:, None] // head_size == jnp.arange(HEADS)[None, :]).astype(jnp.float32)


def head_norm(vector, ones):
    head_size = vector.shape[-1] // HEADS
    sums = jnp.dot(vector * vector, ones, precision=HIGHEST)
    scale = lax.rsqrt(sums / head_size + 1e-06)
    return (vector * jnp.dot(scale, ones.T, precision=HIGHEST)).astype(jnp.bfloat16)


def sublayer(line_rows, w_inner, w_outer):
    feat_len = line_rows.shape[-1]
    head_size = feat_len // HEADS
    ones = head_map(feat_len)
    mask = ones.T.astype(jnp.bfloat16)
    stream = line_rows.astype(jnp.float32)
    normed = (stream * lax.rsqrt(jnp.mean(stream * stream, axis=-1, keepdims=True) + 1e-06)).astype(jnp.bfloat16)
    packed = jnp.dot(normed, w_inner, preferred_element_type=jnp.float32)
    queries = head_norm(packed[..., :feat_len], ones)
    key_part = head_norm(packed[..., feat_len : 2 * feat_len], ones)
    value_part = packed[..., 2 * feat_len :].astype(jnp.bfloat16)
    if line_rows.shape[1] <= 8:
        pairs = queries[:, :, None].astype(jnp.float32) * key_part[:, None].astype(jnp.float32)
        scores = jnp.dot(pairs, ones, precision=HIGHEST) * head_size ** (-0.5)
        powers = jnp.exp(scores)
        attn_weights = (powers / jnp.sum(powers, axis=2, keepdims=True)).astype(jnp.bfloat16)
        spread = jnp.dot(attn_weights, mask, preferred_element_type=jnp.float32)
        mixed_out = jnp.sum(spread * value_part[:, None].astype(jnp.float32), axis=2).astype(jnp.bfloat16)
    else:
        key_heads = key_part[..., None, :] * mask
        scores = jnp.einsum(
            "plqd,pkqhd->pqhlk", queries, key_heads, preferred_element_type=jnp.float32
        ) * head_size ** (-0.5)
        powers = jnp.exp(scores)
        attn_weights = (powers / jnp.sum(powers, axis=-1, keepdims=True)).astype(jnp.bfloat16)
        mixed_heads = jnp.einsum(
            "pqhlk,pkqd->plqhd", attn_weights, value_part, preferred_element_type=jnp.float32
        )
        mixed_out = jnp.sum(mixed_heads * mask.astype(jnp.float32), axis=-2).astype(jnp.bfloat16)
    update = jnp.dot(mixed_out, w_outer, preferred_element_type=jnp.float32)
    return (stream + update).astype(jnp.bfloat16)


def full_weights(w_project, w_output, sizes):
    subs, din, dproj = w_project.shape
    ny = sizes[1]
    source = (lax.axis_index("gy") - jnp.arange(ny)) % ny

    def over_gy(block):
        shifted = [block] + [
            lax.ppermute(block, "gy", [(i, (i + s) % ny) for i in range(ny)]) for s in range(1, ny)
        ]
        rows = jnp.take(jnp.stack(shifted), source, axis=0)
        return jnp.swapaxes(rows, 0, 1).reshape(subs, ny * din, block.shape[2])

    proj = lax.all_gather(over_gy(w_project), ("gz", "gx"), axis=2, tiled=True)
    outp = lax.all_gather(over_gy(w_output), ("gz", "gx"), axis=2, tiled=True)
    return [(proj[i], outp[i]) for i in range(subs)]


def depth_fn(member, w_inner, w_outer):
    depth_len, row_len, rest_len, feat_len = member.shape
    flat_lines = member.reshape(1, depth_len, row_len * rest_len, feat_len)
    return sublayer(flat_lines, w_inner, w_outer).reshape(member.shape)


def plane_fn(plane, w_row, w_col):
    after_rows = sublayer(plane[None], *w_row)[0]
    return sublayer(after_rows[:, :, None, :], *w_col)[:, :, 0, :]


def to_planes(depth_lines, sizes):
    nz, ny, nx = sizes
    z_len, yl, kx, feat = depth_lines.shape
    got = lax.all_to_all(depth_lines, ALL, 0, 0, tiled=True)
    got = got.reshape(nz, ny, nx, yl, kx, feat)
    return jnp.transpose(got, (1, 3, 2, 0, 4, 5)).reshape(ny * yl, nx * nz * kx, feat)


def from_planes(plane, sizes):
    nz, ny, nx = sizes
    rows, cols, feat = plane.shape
    yl, kx = rows // ny, cols // (nx * nz)
    parts = plane.reshape(ny, yl, nx, nz, kx, feat)
    parts = jnp.transpose(parts, (3, 0, 2, 1, 4, 5)).reshape(nz * ny * nx, yl, kx, feat)
    return lax.all_to_all(parts, ALL, 0, 0, tiled=True)


def block_to_plane(block, sizes):
    nz, ny, nx = sizes
    zl, yl, xl, feat = block.shape
    got = lax.all_to_all(block, ("gy", "gx"), 0, 0, tiled=True)
    got = got.reshape(ny, nx, yl, xl, feat)
    return jnp.transpose(got, (0, 2, 1, 3, 4)).reshape(ny * yl, nx * xl, feat)


def local(volume, cotangent, w_project, w_output, sizes):
    w_depth, w_row, w_col = full_weights(w_project, w_output, sizes)

    depth_act = lax.all_to_all(volume, "gz", 2, 0, tiled=True)
    cot_plane = block_to_plane(cotangent, sizes)

    field_one, depth_pullback = jax.vjp(lambda m: depth_fn(m, *w_depth), depth_act)
    plane_one = to_planes(field_one, sizes)
    _, plane_pullback = jax.vjp(lambda p: plane_fn(p, w_row, w_col), plane_one)
    grad_plane = plane_pullback(cot_plane)[0]
    grad_one = from_planes(grad_plane, sizes)
    grad_zero = depth_pullback(grad_one)[0]
    return lax.all_to_all(grad_zero, "gz", 0, 2, tiled=True)


def along_rows(member, w_inner, w_outer):
    return sublayer(member, w_inner, w_outer)


def along_columns(member, w_inner, w_outer):
    depth_len, row_len, col_len, feat_len = member.shape
    flat_lines = member.reshape(depth_len * row_len, col_len, 1, feat_len)
    return sublayer(flat_lines, w_inner, w_outer).reshape(member.shape)


def line_swap(stacked, axis, split_axis, concat_axis):
    return lax.all_to_all(stacked, axis, split_axis=split_axis, concat_axis=concat_axis, tiled=True)


def local_general(volume, cotangent, w_project, w_output, sizes):
    w_depth, w_row, w_col = full_weights(w_project, w_output, sizes)

    def row_fn(member):
        return along_rows(member, *w_row)

    def column_fn(member):
        return along_columns(member, *w_col)

    depth_act = line_swap(volume, "gz", 2, 0)
    field_one, depth_pullback = jax.vjp(lambda m: depth_fn(m, *w_depth), depth_act)
    field_one = line_swap(field_one, "gz", 0, 2)
    row_act = line_swap(field_one, "gy", 2, 1)
    field_two, row_pullback = jax.vjp(row_fn, row_act)
    field_two = line_swap(field_two, "gy", 1, 2)
    paired = line_swap(jnp.stack([cotangent, field_two]), "gx", 1, 3)
    _, column_pullback = jax.vjp(column_fn, paired[1])
    grad_two = line_swap(column_pullback(paired[0])[0], "gx", 2, 0)
    grad_one = line_swap(row_pullback(line_swap(grad_two, "gy", 2, 1))[0], "gy", 1, 2)
    grad_zero = depth_pullback(line_swap(grad_one, "gz", 2, 0))[0]
    return line_swap(grad_zero, "gz", 0, 2)


def solution(mesh):
    sizes = (mesh.shape["gz"], mesh.shape["gy"], mesh.shape["gx"])

    def body(volume, *rest):
        one_depth = volume.shape[0] * sizes[0] == mesh.size
        return (local if one_depth else local_general)(volume, *rest, sizes)

    return jax.shard_map(
        body,
        mesh=mesh,
        in_specs=(
            P("gz", "gy", "gx", None),
            P("gz", "gy", "gx", None),
            P(None, "gy", ("gz", "gx")),
            P(None, "gy", ("gz", "gx")),
        ),
        out_specs=P("gz", "gy", "gx", None),
        check_vma=False,
    )
```

```python
import jax
import jax.numpy as jnp
from jax import lax
from jax.sharding import PartitionSpec as P

HEADS = 6
HIGHEST = lax.Precision.HIGHEST
ALL = ("gz", "gy", "gx")


def head_map(feat_len):
    head_size = feat_len // HEADS
    return (jnp.arange(feat_len)[:, None] // head_size == jnp.arange(HEADS)[None, :]).astype(jnp.float32)


def head_norm(vector, ones):
    head_size = vector.shape[-1] // HEADS
    sums = jnp.dot(vector * vector, ones, precision=HIGHEST)
    scale = lax.rsqrt(sums / head_size + 1e-06)
    return (vector * jnp.dot(scale, ones.T, precision=HIGHEST)).astype(jnp.bfloat16)


def sublayer(line_rows, w_inner, w_outer):
    feat_len = line_rows.shape[-1]
    head_size = feat_len // HEADS
    ones = head_map(feat_len)
    mask = ones.T.astype(jnp.bfloat16)
    stream = line_rows.astype(jnp.float32)
    normed = (stream * lax.rsqrt(jnp.mean(stream * stream, axis=-1, keepdims=True) + 1e-06)).astype(jnp.bfloat16)
    packed = jnp.dot(normed, w_inner, preferred_element_type=jnp.float32)
    queries = head_norm(packed[..., :feat_len], ones)
    key_part = head_norm(packed[..., feat_len : 2 * feat_len], ones)
    value_part = packed[..., 2 * feat_len :].astype(jnp.bfloat16)
    if line_rows.shape[1] <= 8:
        pairs = queries[:, :, None].astype(jnp.float32) * key_part[:, None].astype(jnp.float32)
        scores = jnp.dot(pairs, ones, precision=lax.Precision.HIGH) * head_size ** (-0.5)
        powers = jnp.exp(scores)
        attn_weights = (powers / jnp.sum(powers, axis=2, keepdims=True)).astype(jnp.bfloat16)
        spread = jnp.dot(attn_weights, mask, preferred_element_type=jnp.float32)
        mixed_out = jnp.sum(spread * value_part[:, None].astype(jnp.float32), axis=2).astype(jnp.bfloat16)
    else:
        key_heads = key_part[..., None, :] * mask
        scores = jnp.einsum(
            "plqd,pkqhd->pqhlk", queries, key_heads, preferred_element_type=jnp.float32
        ) * head_size ** (-0.5)
        powers = jnp.exp(scores)
        attn_weights = (powers / jnp.sum(powers, axis=-1, keepdims=True)).astype(jnp.bfloat16)
        mixed_heads = jnp.einsum(
            "pqhlk,pkqd->plqhd", attn_weights, value_part, preferred_element_type=jnp.float32
        )
        mixed_out = jnp.sum(mixed_heads * mask.astype(jnp.float32), axis=-2).astype(jnp.bfloat16)
    update = jnp.dot(mixed_out, w_outer, preferred_element_type=jnp.float32)
    return (stream + update).astype(jnp.bfloat16)


def full_weights(w_project, w_output, sizes):
    subs, din, dproj = w_project.shape
    ny = sizes[1]
    source = (lax.axis_index("gy") - jnp.arange(ny)) % ny

    def over_gy(block):
        shifted = [block] + [
            lax.ppermute(block, "gy", [(i, (i + s) % ny) for i in range(ny)]) for s in range(1, ny)
        ]
        rows = jnp.take(jnp.stack(shifted), source, axis=0)
        return jnp.swapaxes(rows, 0, 1).reshape(subs, ny * din, block.shape[2])

    proj = lax.all_gather(over_gy(w_project), ("gz", "gx"), axis=2, tiled=True)
    outp = lax.all_gather(over_gy(w_output), ("gz", "gx"), axis=2, tiled=True)
    return [(proj[i], outp[i]) for i in range(subs)]


def depth_fn(member, w_inner, w_outer):
    depth_len, row_len, rest_len, feat_len = member.shape
    flat_lines = member.reshape(1, depth_len, row_len * rest_len, feat_len)
    return sublayer(flat_lines, w_inner, w_outer).reshape(member.shape)


def plane_fn(plane, w_row, w_col):
    after_rows = sublayer(plane[None], *w_row)[0]
    return sublayer(after_rows[:, :, None, :], *w_col)[:, :, 0, :]


def to_planes(depth_lines, sizes):
    nz, ny, nx = sizes
    z_len, yl, kx, feat = depth_lines.shape
    got = lax.all_to_all(depth_lines, ALL, 0, 0, tiled=True)
    got = got.reshape(nz, ny, nx, yl, kx, feat)
    return jnp.transpose(got, (1, 3, 2, 0, 4, 5)).reshape(ny * yl, nx * nz * kx, feat)


def from_planes(plane, sizes):
    nz, ny, nx = sizes
    rows, cols, feat = plane.shape
    yl, kx = rows // ny, cols // (nx * nz)
    parts = plane.reshape(ny, yl, nx, nz, kx, feat)
    parts = jnp.transpose(parts, (3, 0, 2, 1, 4, 5)).reshape(nz * ny * nx, yl, kx, feat)
    return lax.all_to_all(parts, ALL, 0, 0, tiled=True)


def block_to_plane(block, sizes):
    nz, ny, nx = sizes
    zl, yl, xl, feat = block.shape
    got = lax.all_to_all(block, ("gy", "gx"), 0, 0, tiled=True)
    got = got.reshape(ny, nx, yl, xl, feat)
    return jnp.transpose(got, (0, 2, 1, 3, 4)).reshape(ny * yl, nx * xl, feat)


def local(volume, cotangent, w_project, w_output, sizes):
    w_depth, w_row, w_col = full_weights(w_project, w_output, sizes)

    depth_act = lax.all_to_all(volume, "gz", 2, 0, tiled=True)
    cot_plane = block_to_plane(cotangent, sizes)

    field_one, depth_pullback = jax.vjp(lambda m: depth_fn(m, *w_depth), depth_act)
    plane_one = to_planes(field_one, sizes)
    _, plane_pullback = jax.vjp(lambda p: plane_fn(p, w_row, w_col), plane_one)
    grad_plane = plane_pullback(cot_plane)[0]
    grad_one = from_planes(grad_plane, sizes)
    grad_zero = depth_pullback(grad_one)[0]
    return lax.all_to_all(grad_zero, "gz", 0, 2, tiled=True)


def along_rows(member, w_inner, w_outer):
    return sublayer(member, w_inner, w_outer)


def along_columns(member, w_inner, w_outer):
    depth_len, row_len, col_len, feat_len = member.shape
    flat_lines = member.reshape(depth_len * row_len, col_len, 1, feat_len)
    return sublayer(flat_lines, w_inner, w_outer).reshape(member.shape)


def line_swap(stacked, axis, split_axis, concat_axis):
    return lax.all_to_all(stacked, axis, split_axis=split_axis, concat_axis=concat_axis, tiled=True)


def local_general(volume, cotangent, w_project, w_output, sizes):
    w_depth, w_row, w_col = full_weights(w_project, w_output, sizes)

    def row_fn(member):
        return along_rows(member, *w_row)

    def column_fn(member):
        return along_columns(member, *w_col)

    depth_act = line_swap(volume, "gz", 2, 0)
    field_one, depth_pullback = jax.vjp(lambda m: depth_fn(m, *w_depth), depth_act)
    field_one = line_swap(field_one, "gz", 0, 2)
    row_act = line_swap(field_one, "gy", 2, 1)
    field_two, row_pullback = jax.vjp(row_fn, row_act)
    field_two = line_swap(field_two, "gy", 1, 2)
    paired = line_swap(jnp.stack([cotangent, field_two]), "gx", 1, 3)
    _, column_pullback = jax.vjp(column_fn, paired[1])
    grad_two = line_swap(column_pullback(paired[0])[0], "gx", 2, 0)
    grad_one = line_swap(row_pullback(line_swap(grad_two, "gy", 2, 1))[0], "gy", 1, 2)
    grad_zero = depth_pullback(line_swap(grad_one, "gz", 2, 0))[0]
    return line_swap(grad_zero, "gz", 0, 2)


def solution(mesh):
    sizes = (mesh.shape["gz"], mesh.shape["gy"], mesh.shape["gx"])

    def body(volume, *rest):
        one_depth = volume.shape[0] * sizes[0] == mesh.size
        return (local if one_depth else local_general)(volume, *rest, sizes)

    return jax.shard_map(
        body,
        mesh=mesh,
        in_specs=(
            P("gz", "gy", "gx", None),
            P("gz", "gy", "gx", None),
            P(None, "gy", ("gz", "gx")),
            P(None, "gy", ("gz", "gx")),
        ),
        out_specs=P("gz", "gy", "gx", None),
        check_vma=False,
    )
```

```python
import jax
import jax.numpy as jnp
from jax import lax
from jax.sharding import PartitionSpec as P

HEADS = 6
HIGHEST = lax.Precision.HIGHEST
ALL = ("gz", "gy", "gx")


def head_map(feat_len):
    head_size = feat_len // HEADS
    return (jnp.arange(feat_len)[:, None] // head_size == jnp.arange(HEADS)[None, :]).astype(jnp.float32)


def head_norm(vector, ones):
    head_size = vector.shape[-1] // HEADS
    sums = jnp.dot(vector * vector, ones, precision=HIGHEST)
    scale = lax.rsqrt(sums / head_size + 1e-06)
    return (vector * jnp.dot(scale, ones.T, precision=lax.Precision.HIGH)).astype(jnp.bfloat16)


def sublayer(line_rows, w_inner, w_outer):
    feat_len = line_rows.shape[-1]
    head_size = feat_len // HEADS
    ones = head_map(feat_len)
    mask = ones.T.astype(jnp.bfloat16)
    stream = line_rows.astype(jnp.float32)
    normed = (stream * lax.rsqrt(jnp.mean(stream * stream, axis=-1, keepdims=True) + 1e-06)).astype(jnp.bfloat16)
    packed = jnp.dot(normed, w_inner, preferred_element_type=jnp.float32)
    queries = head_norm(packed[..., :feat_len], ones)
    key_part = head_norm(packed[..., feat_len : 2 * feat_len], ones)
    value_part = packed[..., 2 * feat_len :].astype(jnp.bfloat16)
    if line_rows.shape[1] <= 8:
        pairs = queries[:, :, None].astype(jnp.float32) * key_part[:, None].astype(jnp.float32)
        scores = jnp.dot(pairs, ones, precision=lax.Precision.HIGH) * head_size ** (-0.5)
        powers = jnp.exp(scores)
        attn_weights = (powers / jnp.sum(powers, axis=2, keepdims=True)).astype(jnp.bfloat16)
        spread = jnp.dot(attn_weights, mask, preferred_element_type=jnp.float32)
        mixed_out = jnp.sum(spread * value_part[:, None].astype(jnp.float32), axis=2).astype(jnp.bfloat16)
    else:
        key_heads = key_part[..., None, :] * mask
        scores = jnp.einsum(
            "plqd,pkqhd->pqhlk", queries, key_heads, preferred_element_type=jnp.float32
        ) * head_size ** (-0.5)
        powers = jnp.exp(scores)
        attn_weights = (powers / jnp.sum(powers, axis=-1, keepdims=True)).astype(jnp.bfloat16)
        mixed_heads = jnp.einsum(
            "pqhlk,pkqd->plqhd", attn_weights, value_part, preferred_element_type=jnp.float32
        )
        mixed_out = jnp.sum(mixed_heads * mask.astype(jnp.float32), axis=-2).astype(jnp.bfloat16)
    update = jnp.dot(mixed_out, w_outer, preferred_element_type=jnp.float32)
    return (stream + update).astype(jnp.bfloat16)


def full_weights(w_project, w_output, sizes):
    subs, din, dproj = w_project.shape
    ny = sizes[1]
    source = (lax.axis_index("gy") - jnp.arange(ny)) % ny

    def over_gy(block):
        shifted = [block] + [
            lax.ppermute(block, "gy", [(i, (i + s) % ny) for i in range(ny)]) for s in range(1, ny)
        ]
        rows = jnp.take(jnp.stack(shifted), source, axis=0)
        return jnp.swapaxes(rows, 0, 1).reshape(subs, ny * din, block.shape[2])

    proj = lax.all_gather(over_gy(w_project), ("gz", "gx"), axis=2, tiled=True)
    outp = lax.all_gather(over_gy(w_output), ("gz", "gx"), axis=2, tiled=True)
    return [(proj[i], outp[i]) for i in range(subs)]


def depth_fn(member, w_inner, w_outer):
    depth_len, row_len, rest_len, feat_len = member.shape
    flat_lines = member.reshape(1, depth_len, row_len * rest_len, feat_len)
    return sublayer(flat_lines, w_inner, w_outer).reshape(member.shape)


def plane_fn(plane, w_row, w_col):
    after_rows = sublayer(plane[None], *w_row)[0]
    return sublayer(after_rows[:, :, None, :], *w_col)[:, :, 0, :]


def to_planes(depth_lines, sizes):
    nz, ny, nx = sizes
    z_len, yl, kx, feat = depth_lines.shape
    got = lax.all_to_all(depth_lines, ALL, 0, 0, tiled=True)
    got = got.reshape(nz, ny, nx, yl, kx, feat)
    return jnp.transpose(got, (1, 3, 2, 0, 4, 5)).reshape(ny * yl, nx * nz * kx, feat)


def from_planes(plane, sizes):
    nz, ny, nx = sizes
    rows, cols, feat = plane.shape
    yl, kx = rows // ny, cols // (nx * nz)
    parts = plane.reshape(ny, yl, nx, nz, kx, feat)
    parts = jnp.transpose(parts, (3, 0, 2, 1, 4, 5)).reshape(nz * ny * nx, yl, kx, feat)
    return lax.all_to_all(parts, ALL, 0, 0, tiled=True)


def block_to_plane(block, sizes):
    nz, ny, nx = sizes
    zl, yl, xl, feat = block.shape
    got = lax.all_to_all(block, ("gy", "gx"), 0, 0, tiled=True)
    got = got.reshape(ny, nx, yl, xl, feat)
    return jnp.transpose(got, (0, 2, 1, 3, 4)).reshape(ny * yl, nx * xl, feat)


def local(volume, cotangent, w_project, w_output, sizes):
    w_depth, w_row, w_col = full_weights(w_project, w_output, sizes)

    depth_act = lax.all_to_all(volume, "gz", 2, 0, tiled=True)
    cot_plane = block_to_plane(cotangent, sizes)

    field_one, depth_pullback = jax.vjp(lambda m: depth_fn(m, *w_depth), depth_act)
    plane_one = to_planes(field_one, sizes)
    _, plane_pullback = jax.vjp(lambda p: plane_fn(p, w_row, w_col), plane_one)
    grad_plane = plane_pullback(cot_plane)[0]
    grad_one = from_planes(grad_plane, sizes)
    grad_zero = depth_pullback(grad_one)[0]
    return lax.all_to_all(grad_zero, "gz", 0, 2, tiled=True)


def along_rows(member, w_inner, w_outer):
    return sublayer(member, w_inner, w_outer)


def along_columns(member, w_inner, w_outer):
    depth_len, row_len, col_len, feat_len = member.shape
    flat_lines = member.reshape(depth_len * row_len, col_len, 1, feat_len)
    return sublayer(flat_lines, w_inner, w_outer).reshape(member.shape)


def line_swap(stacked, axis, split_axis, concat_axis):
    return lax.all_to_all(stacked, axis, split_axis=split_axis, concat_axis=concat_axis, tiled=True)


def local_general(volume, cotangent, w_project, w_output, sizes):
    w_depth, w_row, w_col = full_weights(w_project, w_output, sizes)

    def row_fn(member):
        return along_rows(member, *w_row)

    def column_fn(member):
        return along_columns(member, *w_col)

    depth_act = line_swap(volume, "gz", 2, 0)
    field_one, depth_pullback = jax.vjp(lambda m: depth_fn(m, *w_depth), depth_act)
    field_one = line_swap(field_one, "gz", 0, 2)
    row_act = line_swap(field_one, "gy", 2, 1)
    field_two, row_pullback = jax.vjp(row_fn, row_act)
    field_two = line_swap(field_two, "gy", 1, 2)
    paired = line_swap(jnp.stack([cotangent, field_two]), "gx", 1, 3)
    _, column_pullback = jax.vjp(column_fn, paired[1])
    grad_two = line_swap(column_pullback(paired[0])[0], "gx", 2, 0)
    grad_one = line_swap(row_pullback(line_swap(grad_two, "gy", 2, 1))[0], "gy", 1, 2)
    grad_zero = depth_pullback(line_swap(grad_one, "gz", 2, 0))[0]
    return line_swap(grad_zero, "gz", 0, 2)


def solution(mesh):
    sizes = (mesh.shape["gz"], mesh.shape["gy"], mesh.shape["gx"])

    def body(volume, *rest):
        one_depth = volume.shape[0] * sizes[0] == mesh.size
        return (local if one_depth else local_general)(volume, *rest, sizes)

    return jax.shard_map(
        body,
        mesh=mesh,
        in_specs=(
            P("gz", "gy", "gx", None),
            P("gz", "gy", "gx", None),
            P(None, "gy", ("gz", "gx")),
            P(None, "gy", ("gz", "gx")),
        ),
        out_specs=P("gz", "gy", "gx", None),
        check_vma=False,
    )
```

```python
import jax
import jax.numpy as jnp
from jax import lax
from jax.sharding import PartitionSpec as P

HEADS = 6
HIGHEST = lax.Precision.HIGHEST
ALL = ("gz", "gy", "gx")


def head_map(feat_len):
    head_size = feat_len // HEADS
    return (jnp.arange(feat_len)[:, None] // head_size == jnp.arange(HEADS)[None, :]).astype(jnp.float32)


def head_norm(vector, ones):
    head_size = vector.shape[-1] // HEADS
    sums = jnp.dot(vector * vector, ones, precision=lax.Precision.HIGH)
    scale = lax.rsqrt(sums / head_size + 1e-06)
    return (vector * jnp.dot(scale, ones.T, precision=lax.Precision.HIGH)).astype(jnp.bfloat16)


def sublayer(line_rows, w_inner, w_outer):
    feat_len = line_rows.shape[-1]
    head_size = feat_len // HEADS
    ones = head_map(feat_len)
    mask = ones.T.astype(jnp.bfloat16)
    stream = line_rows.astype(jnp.float32)
    normed = (stream * lax.rsqrt(jnp.mean(stream * stream, axis=-1, keepdims=True) + 1e-06)).astype(jnp.bfloat16)
    packed = jnp.dot(normed, w_inner, preferred_element_type=jnp.float32)
    queries = head_norm(packed[..., :feat_len], ones)
    key_part = head_norm(packed[..., feat_len : 2 * feat_len], ones)
    value_part = packed[..., 2 * feat_len :].astype(jnp.bfloat16)
    if line_rows.shape[1] <= 8:
        pairs = queries[:, :, None].astype(jnp.float32) * key_part[:, None].astype(jnp.float32)
        scores = jnp.dot(pairs, ones, precision=lax.Precision.HIGH) * head_size ** (-0.5)
        powers = jnp.exp(scores)
        attn_weights = (powers / jnp.sum(powers, axis=2, keepdims=True)).astype(jnp.bfloat16)
        spread = jnp.dot(attn_weights, mask, preferred_element_type=jnp.float32)
        mixed_out = jnp.sum(spread * value_part[:, None].astype(jnp.float32), axis=2).astype(jnp.bfloat16)
    else:
        key_heads = key_part[..., None, :] * mask
        scores = jnp.einsum(
            "plqd,pkqhd->pqhlk", queries, key_heads, preferred_element_type=jnp.float32
        ) * head_size ** (-0.5)
        powers = jnp.exp(scores)
        attn_weights = (powers / jnp.sum(powers, axis=-1, keepdims=True)).astype(jnp.bfloat16)
        mixed_heads = jnp.einsum(
            "pqhlk,pkqd->plqhd", attn_weights, value_part, preferred_element_type=jnp.float32
        )
        mixed_out = jnp.sum(mixed_heads * mask.astype(jnp.float32), axis=-2).astype(jnp.bfloat16)
    update = jnp.dot(mixed_out, w_outer, preferred_element_type=jnp.float32)
    return (stream + update).astype(jnp.bfloat16)


def full_weights(w_project, w_output, sizes):
    subs, din, dproj = w_project.shape
    ny = sizes[1]
    source = (lax.axis_index("gy") - jnp.arange(ny)) % ny

    def over_gy(block):
        shifted = [block] + [
            lax.ppermute(block, "gy", [(i, (i + s) % ny) for i in range(ny)]) for s in range(1, ny)
        ]
        rows = jnp.take(jnp.stack(shifted), source, axis=0)
        return jnp.swapaxes(rows, 0, 1).reshape(subs, ny * din, block.shape[2])

    proj = lax.all_gather(over_gy(w_project), ("gz", "gx"), axis=2, tiled=True)
    outp = lax.all_gather(over_gy(w_output), ("gz", "gx"), axis=2, tiled=True)
    return [(proj[i], outp[i]) for i in range(subs)]


def depth_fn(member, w_inner, w_outer):
    depth_len, row_len, rest_len, feat_len = member.shape
    flat_lines = member.reshape(1, depth_len, row_len * rest_len, feat_len)
    return sublayer(flat_lines, w_inner, w_outer).reshape(member.shape)


def plane_fn(plane, w_row, w_col):
    after_rows = sublayer(plane[None], *w_row)[0]
    return sublayer(after_rows[:, :, None, :], *w_col)[:, :, 0, :]


def to_planes(depth_lines, sizes):
    nz, ny, nx = sizes
    z_len, yl, kx, feat = depth_lines.shape
    got = lax.all_to_all(depth_lines, ALL, 0, 0, tiled=True)
    got = got.reshape(nz, ny, nx, yl, kx, feat)
    return jnp.transpose(got, (1, 3, 2, 0, 4, 5)).reshape(ny * yl, nx * nz * kx, feat)


def from_planes(plane, sizes):
    nz, ny, nx = sizes
    rows, cols, feat = plane.shape
    yl, kx = rows // ny, cols // (nx * nz)
    parts = plane.reshape(ny, yl, nx, nz, kx, feat)
    parts = jnp.transpose(parts, (3, 0, 2, 1, 4, 5)).reshape(nz * ny * nx, yl, kx, feat)
    return lax.all_to_all(parts, ALL, 0, 0, tiled=True)


def block_to_plane(block, sizes):
    nz, ny, nx = sizes
    zl, yl, xl, feat = block.shape
    got = lax.all_to_all(block, ("gy", "gx"), 0, 0, tiled=True)
    got = got.reshape(ny, nx, yl, xl, feat)
    return jnp.transpose(got, (0, 2, 1, 3, 4)).reshape(ny * yl, nx * xl, feat)


def local(volume, cotangent, w_project, w_output, sizes):
    w_depth, w_row, w_col = full_weights(w_project, w_output, sizes)

    depth_act = lax.all_to_all(volume, "gz", 2, 0, tiled=True)
    cot_plane = block_to_plane(cotangent, sizes)

    field_one, depth_pullback = jax.vjp(lambda m: depth_fn(m, *w_depth), depth_act)
    plane_one = to_planes(field_one, sizes)
    _, plane_pullback = jax.vjp(lambda p: plane_fn(p, w_row, w_col), plane_one)
    grad_plane = plane_pullback(cot_plane)[0]
    grad_one = from_planes(grad_plane, sizes)
    grad_zero = depth_pullback(grad_one)[0]
    return lax.all_to_all(grad_zero, "gz", 0, 2, tiled=True)


def along_rows(member, w_inner, w_outer):
    return sublayer(member, w_inner, w_outer)


def along_columns(member, w_inner, w_outer):
    depth_len, row_len, col_len, feat_len = member.shape
    flat_lines = member.reshape(depth_len * row_len, col_len, 1, feat_len)
    return sublayer(flat_lines, w_inner, w_outer).reshape(member.shape)


def line_swap(stacked, axis, split_axis, concat_axis):
    return lax.all_to_all(stacked, axis, split_axis=split_axis, concat_axis=concat_axis, tiled=True)


def local_general(volume, cotangent, w_project, w_output, sizes):
    w_depth, w_row, w_col = full_weights(w_project, w_output, sizes)

    def row_fn(member):
        return along_rows(member, *w_row)

    def column_fn(member):
        return along_columns(member, *w_col)

    depth_act = line_swap(volume, "gz", 2, 0)
    field_one, depth_pullback = jax.vjp(lambda m: depth_fn(m, *w_depth), depth_act)
    field_one = line_swap(field_one, "gz", 0, 2)
    row_act = line_swap(field_one, "gy", 2, 1)
    field_two, row_pullback = jax.vjp(row_fn, row_act)
    field_two = line_swap(field_two, "gy", 1, 2)
    paired = line_swap(jnp.stack([cotangent, field_two]), "gx", 1, 3)
    _, column_pullback = jax.vjp(column_fn, paired[1])
    grad_two = line_swap(column_pullback(paired[0])[0], "gx", 2, 0)
    grad_one = line_swap(row_pullback(line_swap(grad_two, "gy", 2, 1))[0], "gy", 1, 2)
    grad_zero = depth_pullback(line_swap(grad_one, "gz", 2, 0))[0]
    return line_swap(grad_zero, "gz", 0, 2)


def solution(mesh):
    sizes = (mesh.shape["gz"], mesh.shape["gy"], mesh.shape["gx"])

    def body(volume, *rest):
        one_depth = volume.shape[0] * sizes[0] == mesh.size
        return (local if one_depth else local_general)(volume, *rest, sizes)

    return jax.shard_map(
        body,
        mesh=mesh,
        in_specs=(
            P("gz", "gy", "gx", None),
            P("gz", "gy", "gx", None),
            P(None, "gy", ("gz", "gx")),
            P(None, "gy", ("gz", "gx")),
        ),
        out_specs=P("gz", "gy", "gx", None),
        check_vma=False,
    )
```
